512 devices in a mesh: ctx: 128 (over z_hi, x, y), head: 4 (over z_lo, core).
Axes of the slice: x: 4, y: 8, z: 8 (z_hi: 4, z_lo: 2; z = z_hi * 2 + z_lo), core: 2. Of those that a mesh axis runs over, the one named last changes fastest.
Arguments:
- queries: bfloat16 [32768, 4096], P(('ctx', 'head')), may hold values from -200 to 200
- normed_key_state: bfloat16 [32768, 2048], P(('ctx', 'head')), may hold values from -5 to 5
- value_state_rows: bfloat16 [32768, 2048], P(('ctx', 'head')), may hold values from -6 to 6
- output_gradient: bfloat16 [32768, 4096], P(('ctx', 'head')), may hold values from -6 to 6
- doc_start: int32 [32768], P('ctx'), may hold values from 0 to 32767, as said below
Outputs:
- grad_queries: bfloat16 [32768, 4096], P(('ctx', 'head'))
- key_gradient: bfloat16 [32768, 2048], P(('ctx', 'head'))
- value_gradient: bfloat16 [32768, 2048], P(('ctx', 'head'))
The draws below stay inside these ranges and needn't reach their ends.
Inputs may be any that keep to these rules, and one draw needn't show every extreme that they name: doc_start[t] is the first position of the document that holds token t: doc_start[0] = 0, each doc_start[t] equals t or doc_start[t - 1], and the last token, position 32767, begins a document of its own.
All inputs are finite; a program needn't handle non-finite values.
Results may differ from the reference program's by a relative error of at most 0.007.
Values may be sent and summed in bfloat16 or wider, within the bound.
No kernel may reach another device: no remote copies, remote signals or barrier semaphores. Data moves between devices by JAX's collectives and lax.ppermute only.
A program may use at most 64 MiB of HBM per device.

```python
import jax
import jax.numpy as jnp
from jax import lax

QUERY_HEADS = 32
KEY_VALUE_HEADS = 16
HEAD_SIZE = 128
WINDOW = 512
TOK_DEV = 256
STREAM_TOKENS = 32768
SPAN = 2


def matched_couple(key):
    base_key = jax.random.fold_in(key, 11)
    subset_keys = jax.random.split(base_key, 2)
    group_share = QUERY_HEADS // KEY_VALUE_HEADS
    unpadded_queries = jnp.clip(jax.random.normal(subset_keys[0], (STREAM_TOKENS, KEY_VALUE_HEADS, group_share, HEAD_SIZE), jnp.float32), -5.0, 5.0)
    unpadded_keys = jnp.clip(jax.random.normal(subset_keys[1], (STREAM_TOKENS, KEY_VALUE_HEADS, HEAD_SIZE), jnp.float32), -5.0, 5.0)
    return (unpadded_queries, unpadded_keys)


def draw_queries(key, part):
    return matched_couple(key)[0].reshape(STREAM_TOKENS, QUERY_HEADS * HEAD_SIZE).astype(jnp.bfloat16)


def draw_normed_key_state(key, part):
    return matched_couple(key)[1].reshape(STREAM_TOKENS, KEY_VALUE_HEADS * HEAD_SIZE).astype(jnp.bfloat16)


def draw_doc_start(key, part):
    base_key = jax.random.fold_in(key, 23)
    level_key, dice_key = jax.random.split(base_key)
    positions = jnp.arange(STREAM_TOKENS, dtype=jnp.int32)
    levels = jax.random.randint(level_key, (STREAM_TOKENS // 256 + 1,), 0, 8)
    dice_rolls = jax.random.randint(dice_key, (STREAM_TOKENS,), 0, 4096)
    starts_here = dice_rolls < jnp.left_shift(jnp.int32(1), levels[positions // 256])
    starts_here = starts_here | (positions == 0) | (positions == STREAM_TOKENS - 1)
    return lax.cummax(jnp.where(starts_here, positions, 0), axis=0).astype(jnp.int32)


def level_of(rng, extent, cuts, low, top_value):
    loudness = 1.0
    for dim, shards_of in cuts:
        heights = jax.random.uniform(jax.random.fold_in(jax.random.fold_in(rng, 6), dim), (shards_of,), jnp.float32, low / len(cuts), top_value / len(cuts))
        loudness = loudness * jnp.repeat(jnp.exp(heights), extent[dim] // shards_of).reshape((-1,) + (1,) * (len(extent) - 1 - dim))
    return loudness


def scatter_about(key, shape, spread, bound, cuts=(), kind=jnp.bfloat16):
    entries = spread * jax.random.normal(key, shape, jnp.float32)
    if cuts:
        entries = entries * level_of(key, shape, cuts, -0.22, 0.18)
    return jnp.clip(entries, -bound, bound).astype(kind)


def setup_inputs(seed: int = 0) -> dict:
    key_of = jax.random.split(jax.random.key(seed), 6)
    queries = draw_queries(jax.random.fold_in(key_of[5], 71), 0)
    normed_key_state = draw_normed_key_state(jax.random.fold_in(key_of[5], 71), 0)
    value_state_rows = scatter_about(key_of[2], (STREAM_TOKENS, KEY_VALUE_HEADS * HEAD_SIZE), 1.0, 6.0, ((0, 512),))
    output_gradient = scatter_about(key_of[3], (STREAM_TOKENS, QUERY_HEADS * HEAD_SIZE), 1.0, 6.0, ((0, 512),))
    doc_start = draw_doc_start(jax.random.fold_in(key_of[5], 71), 0)
    return {"queries": queries, "normed_key_state": normed_key_state, "value_state_rows": value_state_rows, "output_gradient": output_gradient, "doc_start": doc_start}


score_scale = 168.0 ** -0.5
top_prec = lax.Precision.HIGHEST


def round_half(values):
    return lax.optimization_barrier(values.astype(jnp.bfloat16)).astype(jnp.float32)


def reference(queries, normed_key_state, value_state_rows, output_gradient, doc_start):
    group_share = QUERY_HEADS // KEY_VALUE_HEADS
    backward_reach = SPAN * TOK_DEV
    span_rows = backward_reach + TOK_DEV
    num_blocks = STREAM_TOKENS // TOK_DEV
    query_complete = queries.reshape(STREAM_TOKENS, KEY_VALUE_HEADS, group_share, HEAD_SIZE)
    gradient_total = output_gradient.reshape(STREAM_TOKENS, KEY_VALUE_HEADS, group_share, HEAD_SIZE)
    padded_keys = jnp.concatenate([jnp.zeros((backward_reach, KEY_VALUE_HEADS, HEAD_SIZE), normed_key_state.dtype), normed_key_state.reshape(STREAM_TOKENS, KEY_VALUE_HEADS, HEAD_SIZE)], axis=0)
    padded_values = jnp.concatenate([jnp.zeros((backward_reach, KEY_VALUE_HEADS, HEAD_SIZE), value_state_rows.dtype), value_state_rows.reshape(STREAM_TOKENS, KEY_VALUE_HEADS, HEAD_SIZE)], axis=0)

    def one_block(sums_now, block_index):
        key_totals, value_totals = sums_now
        row_start = (block_index * TOK_DEV).astype(jnp.int32)
        query_rows = lax.dynamic_slice_in_dim(query_complete, row_start, TOK_DEV, 0).astype(jnp.float32)
        grad_rows = lax.dynamic_slice_in_dim(gradient_total, row_start, TOK_DEV, 0).astype(jnp.float32)
        key_window = lax.dynamic_slice_in_dim(padded_keys, row_start, span_rows, 0).astype(jnp.float32)
        value_window = lax.dynamic_slice_in_dim(padded_values, row_start, span_rows, 0).astype(jnp.float32)
        first_pos = lax.dynamic_slice_in_dim(doc_start, row_start, TOK_DEV, 0).astype(jnp.int32)
        query_pos = row_start + jnp.arange(TOK_DEV, dtype=jnp.int32)
        key_pos = row_start - backward_reach + jnp.arange(span_rows, dtype=jnp.int32)
        allowed = (key_pos[None, :] >= first_pos[:, None]) & (key_pos[None, :] <= query_pos[:, None]) & (query_pos[:, None] - key_pos[None, :] < WINDOW)
        scores = score_scale * jnp.einsum("tgjd,kgd->gjtk", query_rows, key_window, precision=top_prec)
        masked = jnp.where(allowed, scores, -jnp.inf)
        row_max = jnp.max(masked, axis=-1)
        log_total = row_max + jnp.log(jnp.sum(jnp.exp(masked - row_max[..., None]), axis=-1))
        prob = jnp.exp(masked - log_total[..., None])
        dprob = jnp.einsum("tgjd,kgd->gjtk", grad_rows, value_window, precision=top_prec)
        delta = jnp.sum(prob * dprob, axis=-1)
        dscore = round_half(prob * (dprob - delta[..., None]))
        prob_half = round_half(prob)
        query_grad = score_scale * jnp.einsum("gjtk,kgd->tgjd", dscore, key_window, precision=top_prec)
        key_part = score_scale * jnp.einsum("gjtk,tgjd->kgd", dscore, query_rows, precision=top_prec)
        value_part = jnp.einsum("gjtk,tgjd->kgd", prob_half, grad_rows, precision=top_prec)
        key_totals = lax.dynamic_update_slice_in_dim(key_totals, lax.dynamic_slice_in_dim(key_totals, row_start, span_rows, 0) + key_part, row_start, 0)
        value_totals = lax.dynamic_update_slice_in_dim(value_totals, lax.dynamic_slice_in_dim(value_totals, row_start, span_rows, 0) + value_part, row_start, 0)
        return (key_totals, value_totals), query_grad.reshape(TOK_DEV, QUERY_HEADS * HEAD_SIZE).astype(jnp.bfloat16)

    starting_carry = (jnp.zeros((STREAM_TOKENS + backward_reach, KEY_VALUE_HEADS, HEAD_SIZE), jnp.float32), jnp.zeros((STREAM_TOKENS + backward_reach, KEY_VALUE_HEADS, HEAD_SIZE), jnp.float32))
    (key_totals, value_totals), query_grads = lax.scan(one_block, starting_carry, jnp.arange(num_blocks, dtype=jnp.int32))
    grad_queries = query_grads.reshape(STREAM_TOKENS, QUERY_HEADS * HEAD_SIZE)
    key_gradient = key_totals[backward_reach:].reshape(STREAM_TOKENS, KEY_VALUE_HEADS * HEAD_SIZE).astype(jnp.bfloat16)
    value_gradient = value_totals[backward_reach:].reshape(STREAM_TOKENS, KEY_VALUE_HEADS * HEAD_SIZE).astype(jnp.bfloat16)
    return (grad_queries, key_gradient, value_gradient)
```

```python
import jax
import jax.numpy as jnp
from jax import lax
from jax.sharding import PartitionSpec as P

QUERY_HEADS = 32
KEY_VALUE_HEADS = 16
HEAD_SIZE = 128
WINDOW = 512
SPAN = 2


score_scale = 168.0 ** (-0.5)


def passed_along(block, axis, distance):
    devices = range(lax.axis_size(axis))
    route = [(i - distance, i) for i in devices if i - distance in devices]
    return lax.ppermute(block, axis, route)


def pair_scores(query_heads, key_block):
    return score_scale * jnp.einsum(
        "tgjd,kgd->gjtk", query_heads, key_block, preferred_element_type=jnp.float32
    )


def local(queries, normed_key_state, value_state_rows, output_gradient, doc_start):
    heads_ax = lax.axis_size("head")
    rows_in = queries.shape[0]
    kv_cols = normed_key_state.shape[1] // heads_ax
    q_cols = queries.shape[1] // heads_ax
    kv_in = jnp.stack(
        [
            normed_key_state.reshape(rows_in, heads_ax, kv_cols),
            value_state_rows.reshape(rows_in, heads_ax, kv_cols),
        ],
        axis=2,
    )
    kv_all = lax.all_to_all(kv_in, "head", split_axis=1, concat_axis=0, tiled=True)
    tok_rows = kv_all.shape[0]
    kv_groups = kv_cols // HEAD_SIZE
    group_share = QUERY_HEADS // KEY_VALUE_HEADS
    kv_local = jnp.moveaxis(kv_all[:, 0], 1, 0)
    kv_blocks = [kv_local]
    for distance in range(1, SPAN + 1):
        kv_blocks.append(passed_along(kv_blocks[-1], "ctx", 1))
    qg_in = jnp.stack(
        [
            queries.reshape(rows_in, heads_ax, q_cols),
            output_gradient.reshape(rows_in, heads_ax, q_cols),
        ],
        axis=2,
    )
    qg_all = lax.all_to_all(qg_in, "head", split_axis=1, concat_axis=0, tiled=True)
    query_heads = qg_all[:, 0, 0].reshape(tok_rows, kv_groups, group_share, HEAD_SIZE)
    grad_heads = qg_all[:, 0, 1].reshape(tok_rows, kv_groups, group_share, HEAD_SIZE)
    shard_index = lax.axis_index("ctx")
    local_iota = jnp.arange(tok_rows, dtype=jnp.int32)
    query_pos = shard_index * tok_rows + local_iota

    def visible(distance):
        key_pos = (shard_index - distance) * tok_rows + local_iota
        return (
            (key_pos[None, :] >= doc_start[:, None])
            & (key_pos[None, :] <= query_pos[:, None])
            & (query_pos[:, None] - key_pos[None, :] < WINDOW)
        )

    def unpack(kv_block):
        return (
            kv_block[0].reshape(tok_rows, kv_groups, HEAD_SIZE),
            kv_block[1].reshape(tok_rows, kv_groups, HEAD_SIZE),
        )

    masks = [visible(distance) for distance in range(SPAN + 1)]
    stat_shape = (kv_groups, group_share, tok_rows)
    running = (
        jnp.full(stat_shape, -jnp.inf, jnp.float32),
        jnp.zeros(stat_shape, jnp.float32),
        jnp.zeros(stat_shape, jnp.float32),
    )
    for distance in range(SPAN + 1):
        gather_key_block, gather_value_block = unpack(kv_blocks[distance])
        gather_masked = jnp.where(
            masks[distance], pair_scores(query_heads, gather_key_block), -jnp.inf
        )
        gather_dprob = jnp.einsum(
            "tgjd,kgd->gjtk", grad_heads, gather_value_block, preferred_element_type=jnp.float32
        )
        new_max = jnp.maximum(running[0], jnp.max(gather_masked, axis=-1))
        factor = jnp.exp(running[0] - new_max)
        weights = jnp.exp(gather_masked - new_max[..., None])
        running = (
            new_max,
            running[1] * factor + jnp.sum(weights, axis=-1),
            running[2] * factor + jnp.sum(weights * gather_dprob, axis=-1),
        )
    log_total = running[0] + jnp.log(running[1])
    delta = running[2] / running[1]
    query_total = jnp.zeros((tok_rows, kv_groups, group_share, HEAD_SIZE), jnp.float32)
    kv_parts = {}
    for distance in reversed(range(SPAN + 1)):
        key_block, value_block = unpack(kv_blocks[distance])
        masked = jnp.where(masks[distance], pair_scores(query_heads, key_block), -jnp.inf)
        prob = jnp.exp(masked - log_total[..., None])
        dprob = jnp.einsum(
            "tgjd,kgd->gjtk", grad_heads, value_block, preferred_element_type=jnp.float32
        )
        dscore = (prob * (dprob - delta[..., None])).astype(jnp.bfloat16)
        prob_half = prob.astype(jnp.bfloat16)
        query_part = score_scale * jnp.einsum(
            "gjtk,kgd->tgjd", dscore, key_block, preferred_element_type=jnp.float32
        )
        key_part = score_scale * jnp.einsum(
            "gjtk,tgjd->kgd", dscore, query_heads, preferred_element_type=jnp.float32
        )
        value_part = jnp.einsum(
            "gjtk,tgjd->kgd", prob_half, grad_heads, preferred_element_type=jnp.float32
        )
        query_total = query_total + query_part
        kv_parts[distance] = jnp.stack([key_part, value_part]).reshape(
            2, tok_rows, kv_groups * HEAD_SIZE
        )
    carried = passed_along(kv_parts[2].astype(jnp.bfloat16), "ctx", -1)
    carried = passed_along((kv_parts[1] + carried).astype(jnp.bfloat16), "ctx", -1)
    kv_total = kv_parts[0] + carried
    grad_query_loc = query_total.reshape(tok_rows, kv_groups * group_share * HEAD_SIZE).astype(
        jnp.bfloat16
    )
    grad_q = lax.all_to_all(grad_query_loc, "head", split_axis=0, concat_axis=1, tiled=True)
    kv_out = jnp.moveaxis(kv_total.astype(jnp.bfloat16), 0, 1)[:, None]
    kv_back = lax.all_to_all(kv_out, "head", split_axis=0, concat_axis=1, tiled=True)
    rows_out = kv_back.shape[0]
    grad_k = kv_back[:, :, 0].reshape(rows_out, heads_ax * kv_cols)
    grad_v = kv_back[:, :, 1].reshape(rows_out, heads_ax * kv_cols)
    return grad_q, grad_k, grad_v


def solution(mesh):
    placed = (
        P(("ctx", "head"), None),
        P(("ctx", "head"), None),
        P(("ctx", "head"), None),
        P(("ctx", "head"), None),
        P("ctx"),
    )
    return jax.shard_map(
        local,
        mesh=mesh,
        in_specs=placed,
        out_specs=(P(("ctx", "head"), None), P(("ctx", "head"), None), P(("ctx", "head"), None)),
        check_vma=False,
    )
```

```python
import jax
import jax.numpy as jnp
from jax import lax
from jax.sharding import PartitionSpec as P

QUERY_HEADS = 32
KEY_VALUE_HEADS = 16
HEAD_SIZE = 128
WINDOW = 512
SPAN = 2
CHUNKS = 2
CHAIN = False


score_scale = 168.0 ** (-0.5)


def passed_along(block, axis, distance):
    devices = range(lax.axis_size(axis))
    route = [(i - distance, i) for i in devices if i - distance in devices]
    return lax.ppermute(block, axis, route)


def pair_scores(query_heads, key_block):
    return score_scale * jnp.einsum(
        "tgjd,kgd->gjtk", query_heads, key_block, preferred_element_type=jnp.float32
    )


def attend_chunk(kv_in, qg_in, doc_start):
    kv_all = lax.all_to_all(kv_in, "head", split_axis=1, concat_axis=0, tiled=True)
    tok_rows = kv_all.shape[0]
    kv_cols = kv_all.shape[-1]
    kv_groups = kv_cols // HEAD_SIZE
    group_share = QUERY_HEADS // KEY_VALUE_HEADS
    kv_local = jnp.moveaxis(kv_all[:, 0], 1, 0)
    kv_blocks = [kv_local]
    for distance in range(1, SPAN + 1):
        if CHAIN:
            kv_blocks.append(passed_along(kv_blocks[-1], "ctx", 1))
        else:
            kv_blocks.append(passed_along(kv_local, "ctx", distance))
    qg_all = lax.all_to_all(qg_in, "head", split_axis=1, concat_axis=0, tiled=True)
    query_heads = qg_all[:, 0, 0].reshape(tok_rows, kv_groups, group_share, HEAD_SIZE)
    grad_heads = qg_all[:, 0, 1].reshape(tok_rows, kv_groups, group_share, HEAD_SIZE)
    shard_index = lax.axis_index("ctx")
    local_iota = jnp.arange(tok_rows, dtype=jnp.int32)
    query_pos = shard_index * tok_rows + local_iota

    def visible(distance):
        key_pos = (shard_index - distance) * tok_rows + local_iota
        return (
            (key_pos[None, :] >= doc_start[:, None])
            & (key_pos[None, :] <= query_pos[:, None])
            & (query_pos[:, None] - key_pos[None, :] < WINDOW)
        )

    def unpack(kv_block):
        return (
            kv_block[0].reshape(tok_rows, kv_groups, HEAD_SIZE),
            kv_block[1].reshape(tok_rows, kv_groups, HEAD_SIZE),
        )

    masks = [visible(distance) for distance in range(SPAN + 1)]
    stat_shape = (kv_groups, group_share, tok_rows)
    running = (
        jnp.full(stat_shape, -jnp.inf, jnp.float32),
        jnp.zeros(stat_shape, jnp.float32),
        jnp.zeros(stat_shape, jnp.float32),
    )
    for distance in range(SPAN + 1):
        gather_key_block, gather_value_block = unpack(kv_blocks[distance])
        gather_masked = jnp.where(
            masks[distance], pair_scores(query_heads, gather_key_block), -jnp.inf
        )
        gather_dprob = jnp.einsum(
            "tgjd,kgd->gjtk", grad_heads, gather_value_block, preferred_element_type=jnp.float32
        )
        new_max = jnp.maximum(running[0], jnp.max(gather_masked, axis=-1))
        factor = jnp.exp(running[0] - new_max)
        weights = jnp.exp(gather_masked - new_max[..., None])
        running = (
            new_max,
            running[1] * factor + jnp.sum(weights, axis=-1),
            running[2] * factor + jnp.sum(weights * gather_dprob, axis=-1),
        )
    log_total = running[0] + jnp.log(running[1])
    delta = running[2] / running[1]
    query_total = jnp.zeros((tok_rows, kv_groups, group_share, HEAD_SIZE), jnp.float32)
    kv_parts = {}
    for distance in reversed(range(SPAN + 1)):
        key_block, value_block = unpack(kv_blocks[distance])
        masked = jnp.where(masks[distance], pair_scores(query_heads, key_block), -jnp.inf)
        prob = jnp.exp(masked - log_total[..., None])
        dprob = jnp.einsum(
            "tgjd,kgd->gjtk", grad_heads, value_block, preferred_element_type=jnp.float32
        )
        dscore = (prob * (dprob - delta[..., None])).astype(jnp.bfloat16)
        prob_half = prob.astype(jnp.bfloat16)
        query_part = score_scale * jnp.einsum(
            "gjtk,kgd->tgjd", dscore, key_block, preferred_element_type=jnp.float32
        )
        key_part = score_scale * jnp.einsum(
            "gjtk,tgjd->kgd", dscore, query_heads, preferred_element_type=jnp.float32
        )
        value_part = jnp.einsum(
            "gjtk,tgjd->kgd", prob_half, grad_heads, preferred_element_type=jnp.float32
        )
        query_total = query_total + query_part
        kv_parts[distance] = jnp.stack([key_part, value_part]).reshape(2, tok_rows, kv_cols)
    if CHAIN:
        carried = passed_along(kv_parts[2].astype(jnp.bfloat16), "ctx", -1)
        carried = passed_along((kv_parts[1] + carried).astype(jnp.bfloat16), "ctx", -1)
        kv_total = kv_parts[0] + carried
    else:
        kv_total = kv_parts[0]
        for distance in range(1, SPAN + 1):
            kv_total = kv_total + passed_along(
                kv_parts[distance].astype(jnp.bfloat16), "ctx", -distance
            )
    grad_query_loc = query_total.reshape(tok_rows, 1, kv_groups * group_share * HEAD_SIZE)
    grad_q = lax.all_to_all(
        grad_query_loc.astype(jnp.bfloat16), "head", split_axis=0, concat_axis=1, tiled=True
    )
    kv_out = jnp.moveaxis(kv_total.astype(jnp.bfloat16), 0, 1)[:, None]
    kv_back = lax.all_to_all(kv_out, "head", split_axis=0, concat_axis=1, tiled=True)
    return grad_q, kv_back


def local(queries, normed_key_state, value_state_rows, output_gradient, doc_start):
    heads_ax = lax.axis_size("head")
    rows_in = queries.shape[0]
    kv_cols = normed_key_state.shape[1] // (heads_ax * CHUNKS)
    q_cols = queries.shape[1] // (heads_ax * CHUNKS)
    keys = normed_key_state.reshape(rows_in, heads_ax, CHUNKS, kv_cols)
    values = value_state_rows.reshape(rows_in, heads_ax, CHUNKS, kv_cols)
    qs = queries.reshape(rows_in, heads_ax, CHUNKS, q_cols)
    gs = output_gradient.reshape(rows_in, heads_ax, CHUNKS, q_cols)
    dq_parts, dkv_parts = [], []
    for chunk in range(CHUNKS):
        kv_in = jnp.stack([keys[:, :, chunk], values[:, :, chunk]], axis=2)
        qg_in = jnp.stack([qs[:, :, chunk], gs[:, :, chunk]], axis=2)
        dq, dkv = attend_chunk(kv_in, qg_in, doc_start)
        dq_parts.append(dq)
        dkv_parts.append(dkv)
    grad_q = jnp.stack(dq_parts, axis=2).reshape(rows_in, heads_ax * CHUNKS * q_cols)
    dkv = jnp.stack(dkv_parts, axis=3)
    grad_k = dkv[:, :, 0].reshape(rows_in, heads_ax * CHUNKS * kv_cols)
    grad_v = dkv[:, :, 1].reshape(rows_in, heads_ax * CHUNKS * kv_cols)
    return grad_q, grad_k, grad_v


def solution(mesh):
    placed = (
        P(("ctx", "head"), None),
        P(("ctx", "head"), None),
        P(("ctx", "head"), None),
        P(("ctx", "head"), None),
        P("ctx"),
    )
    return jax.shard_map(
        local,
        mesh=mesh,
        in_specs=placed,
        out_specs=(P(("ctx", "head"), None), P(("ctx", "head"), None), P(("ctx", "head"), None)),
        check_vma=False,
    )
```

```python
import jax
import jax.numpy as jnp
from jax import lax
from jax.experimental import pallas as pl
from jax.sharding import PartitionSpec as P

QUERY_HEADS = 32
KEY_VALUE_HEADS = 16
HEAD_SIZE = 128
WINDOW = 512
SPAN = 2
CHAIN = False

score_scale = 168.0 ** (-0.5)
NT = (((1,), (1,)), ((), ()))
TN = (((0,), (0,)), ((), ()))


def attn_kernel(rel_ref, q_ref, g_ref, kv0_ref, kv1_ref, kv2_ref, dq_ref, dkv0_ref, dkv1_ref, dkv2_ref):
    tok = q_ref.shape[0]
    kv_refs = (kv0_ref, kv1_ref, kv2_ref)
    dkv_refs = (dkv0_ref, dkv1_ref, dkv2_ref)
    share = q_ref.shape[1] // HEAD_SIZE
    row = lax.broadcasted_iota(jnp.int32, (tok, tok), 0)
    col = lax.broadcasted_iota(jnp.int32, (tok, tok), 1)
    rel = rel_ref[...]
    masks = []
    for d in range(3):
        key_rel = col - tok * d
        masks.append((key_rel >= rel) & (key_rel <= row) & (row - key_rel < WINDOW))
    keys = [r[0] for r in kv_refs]
    vals = [r[1] for r in kv_refs]
    dk = [jnp.zeros((tok, HEAD_SIZE), jnp.float32) for _ in range(3)]
    dv = [jnp.zeros((tok, HEAD_SIZE), jnp.float32) for _ in range(3)]
    for j in range(share):
        qj = q_ref[:, j * HEAD_SIZE:(j + 1) * HEAD_SIZE]
        gj = g_ref[:, j * HEAD_SIZE:(j + 1) * HEAD_SIZE]
        scores = []
        for d in range(3):
            s = score_scale * lax.dot_general(qj, keys[d], NT, preferred_element_type=jnp.float32)
            scores.append(jnp.where(masks[d], s, -jnp.inf))
        m = jnp.max(scores[0], axis=1, keepdims=True)
        for d in range(1, 3):
            m = jnp.maximum(m, jnp.max(scores[d], axis=1, keepdims=True))
        tot = jnp.zeros_like(m)
        for d in range(3):
            tot = tot + jnp.sum(jnp.exp(scores[d] - m), axis=1, keepdims=True)
        lse = m + jnp.log(tot)
        probs, dprobs = [], []
        delta = jnp.zeros_like(m)
        for d in range(3):
            p = jnp.exp(scores[d] - lse)
            dp = lax.dot_general(gj, vals[d], NT, preferred_element_type=jnp.float32)
            delta = delta + jnp.sum(p * dp, axis=1, keepdims=True)
            probs.append(p)
            dprobs.append(dp)
        dq = jnp.zeros((tok, HEAD_SIZE), jnp.float32)
        for d in range(3):
            ds = (probs[d] * (dprobs[d] - delta)).astype(jnp.bfloat16)
            ph = probs[d].astype(jnp.bfloat16)
            dq = dq + jnp.dot(ds, keys[d], preferred_element_type=jnp.float32)
            dk[d] = dk[d] + lax.dot_general(ds, qj, TN, preferred_element_type=jnp.float32)
            dv[d] = dv[d] + lax.dot_general(ph, gj, TN, preferred_element_type=jnp.float32)
        dq_ref[:, j * HEAD_SIZE:(j + 1) * HEAD_SIZE] = score_scale * dq
    for d in range(3):
        dkv_refs[d][0] = score_scale * dk[d]
        dkv_refs[d][1] = dv[d]


def attend(rel, qh, gh, kv_blocks):
    tok, qcols = qh.shape
    kvcols = kv_blocks[0].shape[-1]
    groups = kvcols // HEAD_SIZE
    qblk = qcols // groups
    kv_spec = pl.BlockSpec((2, tok, HEAD_SIZE), lambda g: (0, 0, g))
    q_spec = pl.BlockSpec((tok, qblk), lambda g: (0, g))
    return pl.pallas_call(
        attn_kernel,
        grid=(groups,),
        in_specs=[pl.BlockSpec((tok, 1), lambda g: (0, 0)), q_spec, q_spec, kv_spec, kv_spec, kv_spec],
        out_specs=[q_spec, kv_spec, kv_spec, kv_spec],
        out_shape=[
            jax.ShapeDtypeStruct((tok, qcols), jnp.float32),
            jax.ShapeDtypeStruct((2, tok, kvcols), jnp.float32),
            jax.ShapeDtypeStruct((2, tok, kvcols), jnp.float32),
            jax.ShapeDtypeStruct((2, tok, kvcols), jnp.float32),
        ],
    )(rel, qh, gh, *kv_blocks)


def passed_along(block, axis, distance):
    devices = range(lax.axis_size(axis))
    route = [(i - distance, i) for i in devices if i - distance in devices]
    return lax.ppermute(block, axis, route)


def local(queries, normed_key_state, value_state_rows, output_gradient, doc_start):
    heads_ax = lax.axis_size("head")
    rows_in = queries.shape[0]
    kv_cols = normed_key_state.shape[1] // heads_ax
    q_cols = queries.shape[1] // heads_ax
    kv_in = jnp.stack(
        [
            normed_key_state.reshape(rows_in, heads_ax, kv_cols),
            value_state_rows.reshape(rows_in, heads_ax, kv_cols),
        ],
        axis=2,
    )
    kv_all = lax.all_to_all(kv_in, "head", split_axis=1, concat_axis=0, tiled=True)
    tok_rows = kv_all.shape[0]
    kv_local = jnp.moveaxis(kv_all[:, 0], 1, 0)
    kv_blocks = [kv_local]
    for distance in range(1, SPAN + 1):
        if CHAIN:
            kv_blocks.append(passed_along(kv_blocks[-1], "ctx", 1))
        else:
            kv_blocks.append(passed_along(kv_local, "ctx", distance))
    qg_in = jnp.stack(
        [
            queries.reshape(rows_in, heads_ax, q_cols),
            output_gradient.reshape(rows_in, heads_ax, q_cols),
        ],
        axis=2,
    )
    qg_all = lax.all_to_all(qg_in, "head", split_axis=1, concat_axis=0, tiled=True)
    shard_index = lax.axis_index("ctx")
    rel = (doc_start - shard_index * tok_rows).reshape(tok_rows, 1)
    dq, dkv0, dkv1, dkv2 = attend(rel, qg_all[:, 0, 0], qg_all[:, 0, 1], kv_blocks)
    if CHAIN:
        carried = passed_along(dkv2.astype(jnp.bfloat16), "ctx", -1)
        carried = passed_along((dkv1 + carried).astype(jnp.bfloat16), "ctx", -1)
        kv_total = dkv0 + carried
    else:
        kv_total = dkv0
        for distance, part in ((1, dkv1), (2, dkv2)):
            kv_total = kv_total + passed_along(part.astype(jnp.bfloat16), "ctx", -distance)
    grad_q = lax.all_to_all(
        dq.astype(jnp.bfloat16)[:, None], "head", split_axis=0, concat_axis=1, tiled=True
    ).reshape(rows_in, heads_ax * q_cols)
    kv_out = jnp.moveaxis(kv_total.astype(jnp.bfloat16), 0, 1)[:, None]
    kv_back = lax.all_to_all(kv_out, "head", split_axis=0, concat_axis=1, tiled=True)
    grad_k = kv_back[:, :, 0].reshape(rows_in, heads_ax * kv_cols)
    grad_v = kv_back[:, :, 1].reshape(rows_in, heads_ax * kv_cols)
    return grad_q, grad_k, grad_v


def solution(mesh):
    placed = (
        P(("ctx", "head"), None),
        P(("ctx", "head"), None),
        P(("ctx", "head"), None),
        P(("ctx", "head"), None),
        P("ctx"),
    )
    return jax.shard_map(
        local,
        mesh=mesh,
        in_specs=placed,
        out_specs=(P(("ctx", "head"), None), P(("ctx", "head"), None), P(("ctx", "head"), None)),
        check_vma=False,
    )
```

```python
import jax
import jax.numpy as jnp
from jax import lax
from jax.experimental import pallas as pl
from jax.sharding import PartitionSpec as P

QUERY_HEADS = 32
KEY_VALUE_HEADS = 16
HEAD_SIZE = 128
WINDOW = 512
SPAN = 2
CHAIN = False
CHUNKS = 2

score_scale = 168.0 ** (-0.5)
NT = (((1,), (1,)), ((), ()))
TN = (((0,), (0,)), ((), ()))


def attn_kernel(rel_ref, q_ref, g_ref, kv0_ref, kv1_ref, kv2_ref, dq_ref, dkv0_ref, dkv1_ref, dkv2_ref):
    tok = q_ref.shape[0]
    kv_refs = (kv0_ref, kv1_ref, kv2_ref)
    dkv_refs = (dkv0_ref, dkv1_ref, dkv2_ref)
    share = q_ref.shape[1] // HEAD_SIZE
    row = lax.broadcasted_iota(jnp.int32, (tok, tok), 0)
    col = lax.broadcasted_iota(jnp.int32, (tok, tok), 1)
    rel = rel_ref[...]
    masks = []
    for d in range(3):
        key_rel = col - tok * d
        masks.append((key_rel >= rel) & (key_rel <= row) & (row - key_rel < WINDOW))
    keys = [r[0] for r in kv_refs]
    vals = [r[1] for r in kv_refs]
    dk = [jnp.zeros((tok, HEAD_SIZE), jnp.float32) for _ in range(3)]
    dv = [jnp.zeros((tok, HEAD_SIZE), jnp.float32) for _ in range(3)]
    for j in range(share):
        qj = q_ref[:, j * HEAD_SIZE:(j + 1) * HEAD_SIZE]
        gj = g_ref[:, j * HEAD_SIZE:(j + 1) * HEAD_SIZE]
        scores = []
        for d in range(3):
            s = score_scale * lax.dot_general(qj, keys[d], NT, preferred_element_type=jnp.float32)
            scores.append(jnp.where(masks[d], s, -jnp.inf))
        m = jnp.max(scores[0], axis=1, keepdims=True)
        for d in range(1, 3):
            m = jnp.maximum(m, jnp.max(scores[d], axis=1, keepdims=True))
        tot = jnp.zeros_like(m)
        for d in range(3):
            tot = tot + jnp.sum(jnp.exp(scores[d] - m), axis=1, keepdims=True)
        lse = m + jnp.log(tot)
        probs, dprobs = [], []
        delta = jnp.zeros_like(m)
        for d in range(3):
            p = jnp.exp(scores[d] - lse)
            dp = lax.dot_general(gj, vals[d], NT, preferred_element_type=jnp.float32)
            delta = delta + jnp.sum(p * dp, axis=1, keepdims=True)
            probs.append(p)
            dprobs.append(dp)
        dq = jnp.zeros((tok, HEAD_SIZE), jnp.float32)
        for d in range(3):
            ds = (probs[d] * (dprobs[d] - delta)).astype(jnp.bfloat16)
            ph = probs[d].astype(jnp.bfloat16)
            dq = dq + jnp.dot(ds, keys[d], preferred_element_type=jnp.float32)
            dk[d] = dk[d] + lax.dot_general(ds, qj, TN, preferred_element_type=jnp.float32)
            dv[d] = dv[d] + lax.dot_general(ph, gj, TN, preferred_element_type=jnp.float32)
        dq_ref[:, j * HEAD_SIZE:(j + 1) * HEAD_SIZE] = score_scale * dq
    for d in range(3):
        dkv_refs[d][0] = score_scale * dk[d]
        dkv_refs[d][1] = dv[d]


def attend(rel, qh, gh, kv_blocks):
    tok, qcols = qh.shape
    kvcols = kv_blocks[0].shape[-1]
    groups = kvcols // HEAD_SIZE
    qblk = qcols // groups
    kv_spec = pl.BlockSpec((2, tok, HEAD_SIZE), lambda g: (0, 0, g))
    q_spec = pl.BlockSpec((tok, qblk), lambda g: (0, g))
    return pl.pallas_call(
        attn_kernel,
        grid=(groups,),
        in_specs=[pl.BlockSpec((tok, 1), lambda g: (0, 0)), q_spec, q_spec, kv_spec, kv_spec, kv_spec],
        out_specs=[q_spec, kv_spec, kv_spec, kv_spec],
        out_shape=[
            jax.ShapeDtypeStruct((tok, qcols), jnp.float32),
            jax.ShapeDtypeStruct((2, tok, kvcols), jnp.float32),
            jax.ShapeDtypeStruct((2, tok, kvcols), jnp.float32),
            jax.ShapeDtypeStruct((2, tok, kvcols), jnp.float32),
        ],
    )(rel, qh, gh, *kv_blocks)


def passed_along(block, axis, distance):
    devices = range(lax.axis_size(axis))
    route = [(i - distance, i) for i in devices if i - distance in devices]
    return lax.ppermute(block, axis, route)


def chunk_pass(kv_in, qg_in, rel):
    kv_all = lax.all_to_all(kv_in, "head", split_axis=1, concat_axis=0, tiled=True)
    kv_local = jnp.moveaxis(kv_all[:, 0], 1, 0)
    kv_blocks = [kv_local]
    for distance in range(1, SPAN + 1):
        if CHAIN:
            kv_blocks.append(passed_along(kv_blocks[-1], "ctx", 1))
        else:
            kv_blocks.append(passed_along(kv_local, "ctx", distance))
    qg_all = lax.all_to_all(qg_in, "head", split_axis=1, concat_axis=0, tiled=True)
    dq, dkv0, dkv1, dkv2 = attend(rel, qg_all[:, 0, 0], qg_all[:, 0, 1], kv_blocks)
    if CHAIN:
        carried = passed_along(dkv2.astype(jnp.bfloat16), "ctx", -1)
        carried = passed_along((dkv1 + carried).astype(jnp.bfloat16), "ctx", -1)
        kv_total = dkv0 + carried
    else:
        kv_total = dkv0
        for distance, part in ((1, dkv1), (2, dkv2)):
            kv_total = kv_total + passed_along(part.astype(jnp.bfloat16), "ctx", -distance)
    grad_q = lax.all_to_all(
        dq.astype(jnp.bfloat16)[:, None], "head", split_axis=0, concat_axis=1, tiled=True
    )
    kv_out = jnp.moveaxis(kv_total.astype(jnp.bfloat16), 0, 1)[:, None]
    kv_back = lax.all_to_all(kv_out, "head", split_axis=0, concat_axis=1, tiled=True)
    return grad_q, kv_back


def local(queries, normed_key_state, value_state_rows, output_gradient, doc_start):
    heads_ax = lax.axis_size("head")
    rows_in = queries.shape[0]
    tok_rows = doc_start.shape[0]
    kv_cols = normed_key_state.shape[1] // (heads_ax * CHUNKS)
    q_cols = queries.shape[1] // (heads_ax * CHUNKS)
    keys = normed_key_state.reshape(rows_in, heads_ax, CHUNKS, kv_cols)
    values = value_state_rows.reshape(rows_in, heads_ax, CHUNKS, kv_cols)
    qs = queries.reshape(rows_in, heads_ax, CHUNKS, q_cols)
    gs = output_gradient.reshape(rows_in, heads_ax, CHUNKS, q_cols)
    shard_index = lax.axis_index("ctx")
    rel = (doc_start - shard_index * tok_rows).reshape(tok_rows, 1)
    dq_parts, dkv_parts = [], []
    for chunk in range(CHUNKS):
        kv_in = jnp.stack([keys[:, :, chunk], values[:, :, chunk]], axis=2)
        qg_in = jnp.stack([qs[:, :, chunk], gs[:, :, chunk]], axis=2)
        dq, dkv = chunk_pass(kv_in, qg_in, rel)
        dq_parts.append(dq)
        dkv_parts.append(dkv)
    grad_q = jnp.stack(dq_parts, axis=2).reshape(rows_in, heads_ax * CHUNKS * q_cols)
    dkv = jnp.stack(dkv_parts, axis=3)
    grad_k = dkv[:, :, 0].reshape(rows_in, heads_ax * CHUNKS * kv_cols)
    grad_v = dkv[:, :, 1].reshape(rows_in, heads_ax * CHUNKS * kv_cols)
    return grad_q, grad_k, grad_v


def solution(mesh):
    placed = (
        P(("ctx", "head"), None),
        P(("ctx", "head"), None),
        P(("ctx", "head"), None),
        P(("ctx", "head"), None),
        P("ctx"),
    )
    return jax.shard_map(
        local,
        mesh=mesh,
        in_specs=placed,
        out_specs=(P(("ctx", "head"), None), P(("ctx", "head"), None), P(("ctx", "head"), None)),
        check_vma=False,
    )
```

```python
import jax
import jax.numpy as jnp
from jax import lax
from jax.experimental import pallas as pl
from jax.sharding import PartitionSpec as P

QUERY_HEADS = 32
KEY_VALUE_HEADS = 16
HEAD_SIZE = 128
WINDOW = 512
SPAN = 2
CHAIN = False

score_scale = 168.0 ** (-0.5)
NT = (((1,), (1,)), ((), ()))
TN = (((0,), (0,)), ((), ()))


def attn_kernel(rel_ref, q_ref, g_ref, k0_ref, v0_ref, k1_ref, v1_ref, k2_ref, v2_ref, dq_ref, dkv0_ref, dkv1_ref, dkv2_ref):
    tok = q_ref.shape[0]
    dkv_refs = (dkv0_ref, dkv1_ref, dkv2_ref)
    share = q_ref.shape[1] // HEAD_SIZE
    row = lax.broadcasted_iota(jnp.int32, (tok, tok), 0)
    col = lax.broadcasted_iota(jnp.int32, (tok, tok), 1)
    rel = rel_ref[...]
    masks = []
    for d in range(3):
        key_rel = col - tok * d
        masks.append((key_rel >= rel) & (key_rel <= row) & (row - key_rel < WINDOW))
    keys = [k0_ref[...], k1_ref[...], k2_ref[...]]
    vals = [v0_ref[...], v1_ref[...], v2_ref[...]]
    dk = [jnp.zeros((tok, HEAD_SIZE), jnp.float32) for _ in range(3)]
    dv = [jnp.zeros((tok, HEAD_SIZE), jnp.float32) for _ in range(3)]
    for j in range(share):
        qj = q_ref[:, j * HEAD_SIZE:(j + 1) * HEAD_SIZE]
        gj = g_ref[:, j * HEAD_SIZE:(j + 1) * HEAD_SIZE]
        scores = []
        for d in range(3):
            s = score_scale * lax.dot_general(qj, keys[d], NT, preferred_element_type=jnp.float32)
            scores.append(jnp.where(masks[d], s, -jnp.inf))
        m = jnp.max(scores[0], axis=1, keepdims=True)
        for d in range(1, 3):
            m = jnp.maximum(m, jnp.max(scores[d], axis=1, keepdims=True))
        tot = jnp.zeros_like(m)
        for d in range(3):
            tot = tot + jnp.sum(jnp.exp(scores[d] - m), axis=1, keepdims=True)
        lse = m + jnp.log(tot)
        probs, dprobs = [], []
        delta = jnp.zeros_like(m)
        for d in range(3):
            p = jnp.exp(scores[d] - lse)
            dp = lax.dot_general(gj, vals[d], NT, preferred_element_type=jnp.float32)
            delta = delta + jnp.sum(p * dp, axis=1, keepdims=True)
            probs.append(p)
            dprobs.append(dp)
        dq = jnp.zeros((tok, HEAD_SIZE), jnp.float32)
        for d in range(3):
            ds = (probs[d] * (dprobs[d] - delta)).astype(jnp.bfloat16)
            ph = probs[d].astype(jnp.bfloat16)
            dq = dq + jnp.dot(ds, keys[d], preferred_element_type=jnp.float32)
            dk[d] = dk[d] + lax.dot_general(ds, qj, TN, preferred_element_type=jnp.float32)
            dv[d] = dv[d] + lax.dot_general(ph, gj, TN, preferred_element_type=jnp.float32)
        dq_ref[:, j * HEAD_SIZE:(j + 1) * HEAD_SIZE] = score_scale * dq
    for d in range(3):
        dkv_refs[d][0] = score_scale * dk[d]
        dkv_refs[d][1] = dv[d]


def attend(rel, x_all, kv_blocks):
    tok = x_all.shape[0]
    kvcols = kv_blocks[0].shape[1] // 2
    groups = kvcols // HEAD_SIZE
    qblk = 2 * kvcols // groups
    col = lambda off: pl.BlockSpec((tok, HEAD_SIZE), lambda g: (0, off + g))
    qcol = lambda off: pl.BlockSpec((tok, qblk), lambda g: (0, off + g))
    kv_spec = pl.BlockSpec((2, tok, HEAD_SIZE), lambda g: (0, 0, g))
    return pl.pallas_call(
        attn_kernel,
        grid=(groups,),
        in_specs=[
            pl.BlockSpec((tok, 1), lambda g: (0, 0)),
            qcol(2 * kvcols // qblk),
            qcol(4 * kvcols // qblk),
            col(0),
            col(groups),
            col(0),
            col(groups),
            col(0),
            col(groups),
        ],
        out_specs=[pl.BlockSpec((tok, qblk), lambda g: (0, g)), kv_spec, kv_spec, kv_spec],
        out_shape=[
            jax.ShapeDtypeStruct((tok, 2 * kvcols), jnp.float32),
            jax.ShapeDtypeStruct((2, tok, kvcols), jnp.float32),
            jax.ShapeDtypeStruct((2, tok, kvcols), jnp.float32),
            jax.ShapeDtypeStruct((2, tok, kvcols), jnp.float32),
        ],
    )(rel, x_all, x_all, x_all, x_all, kv_blocks[0], kv_blocks[0], kv_blocks[1], kv_blocks[1])


def passed_along(block, axis, distance):
    devices = range(lax.axis_size(axis))
    route = [(i - distance, i) for i in devices if i - distance in devices]
    return lax.ppermute(block, axis, route)


def local(queries, normed_key_state, value_state_rows, output_gradient, doc_start):
    heads_ax = lax.axis_size("head")
    rows_in = queries.shape[0]
    tok_rows = doc_start.shape[0]
    kv_cols = normed_key_state.shape[1] // heads_ax
    q_cols = queries.shape[1] // heads_ax
    x_in = jnp.concatenate(
        [
            normed_key_state.reshape(rows_in, heads_ax, kv_cols),
            value_state_rows.reshape(rows_in, heads_ax, kv_cols),
            queries.reshape(rows_in, heads_ax, q_cols),
            output_gradient.reshape(rows_in, heads_ax, q_cols),
        ],
        axis=2,
    )
    x_all = lax.all_to_all(x_in, "head", split_axis=1, concat_axis=0, tiled=True)
    x_all = x_all.reshape(tok_rows, 2 * kv_cols + 2 * q_cols)
    kv_local = x_all[:, : 2 * kv_cols]
    if CHAIN:
        kv1 = passed_along(kv_local, "ctx", 1)
        kv2 = passed_along(kv1, "ctx", 1)
    else:
        kv1 = passed_along(kv_local, "ctx", 1)
        kv2 = passed_along(kv_local, "ctx", 2)
    shard_index = lax.axis_index("ctx")
    rel = (doc_start - shard_index * tok_rows).reshape(tok_rows, 1)
    dq, dkv0, dkv1, dkv2 = attend(rel, x_all, (kv1, kv2))
    if CHAIN:
        carried = passed_along(dkv2.astype(jnp.bfloat16), "ctx", -1)
        carried = passed_along((dkv1 + carried).astype(jnp.bfloat16), "ctx", -1)
        kv_total = dkv0 + carried
    else:
        kv_total = dkv0
        for distance, part in ((1, dkv1), (2, dkv2)):
            kv_total = kv_total + passed_along(part.astype(jnp.bfloat16), "ctx", -distance)
    out_loc = jnp.concatenate(
        [dq.astype(jnp.bfloat16), kv_total[0].astype(jnp.bfloat16), kv_total[1].astype(jnp.bfloat16)],
        axis=1,
    )[:, None]
    out = lax.all_to_all(out_loc, "head", split_axis=0, concat_axis=1, tiled=True)
    grad_q = out[:, :, :q_cols].reshape(rows_in, heads_ax * q_cols)
    grad_k = out[:, :, q_cols : q_cols + kv_cols].reshape(rows_in, heads_ax * kv_cols)
    grad_v = out[:, :, q_cols + kv_cols :].reshape(rows_in, heads_ax * kv_cols)
    return grad_q, grad_k, grad_v


def solution(mesh):
    placed = (
        P(("ctx", "head"), None),
        P(("ctx", "head"), None),
        P(("ctx", "head"), None),
        P(("ctx", "head"), None),
        P("ctx"),
    )
    return jax.shard_map(
        local,
        mesh=mesh,
        in_specs=placed,
        out_specs=(P(("ctx", "head"), None), P(("ctx", "head"), None), P(("ctx", "head"), None)),
        check_vma=False,
    )
```

```python
import jax
import jax.numpy as jnp
from jax import lax
from jax.experimental import pallas as pl
from jax.sharding import PartitionSpec as P

QUERY_HEADS = 32
KEY_VALUE_HEADS = 16
HEAD_SIZE = 128
WINDOW = 512
SPAN = 2
CHAIN = False
CHUNKS = 2

score_scale = 168.0 ** (-0.5)
NT = (((1,), (1,)), ((), ()))
TN = (((0,), (0,)), ((), ()))


def attn_kernel(rel_ref, q_ref, g_ref, k0_ref, v0_ref, k1_ref, v1_ref, k2_ref, v2_ref, dq_ref, dkv0_ref, dkv1_ref, dkv2_ref):
    tok = q_ref.shape[0]
    dkv_refs = (dkv0_ref, dkv1_ref, dkv2_ref)
    share = q_ref.shape[1] // HEAD_SIZE
    row = lax.broadcasted_iota(jnp.int32, (tok, tok), 0)
    col = lax.broadcasted_iota(jnp.int32, (tok, tok), 1)
    rel = rel_ref[...]
    masks = []
    for d in range(3):
        key_rel = col - tok * d
        masks.append((key_rel >= rel) & (key_rel <= row) & (row - key_rel < WINDOW))
    keys = [k0_ref[...], k1_ref[...], k2_ref[...]]
    vals = [v0_ref[...], v1_ref[...], v2_ref[...]]
    dk = [jnp.zeros((tok, HEAD_SIZE), jnp.float32) for _ in range(3)]
    dv = [jnp.zeros((tok, HEAD_SIZE), jnp.float32) for _ in range(3)]
    for j in range(share):
        qj = q_ref[:, j * HEAD_SIZE:(j + 1) * HEAD_SIZE]
        gj = g_ref[:, j * HEAD_SIZE:(j + 1) * HEAD_SIZE]
        scores = []
        for d in range(3):
            s = score_scale * lax.dot_general(qj, keys[d], NT, preferred_element_type=jnp.float32)
            scores.append(jnp.where(masks[d], s, -jnp.inf))
        m = jnp.max(scores[0], axis=1, keepdims=True)
        for d in range(1, 3):
            m = jnp.maximum(m, jnp.max(scores[d], axis=1, keepdims=True))
        tot = jnp.zeros_like(m)
        for d in range(3):
            tot = tot + jnp.sum(jnp.exp(scores[d] - m), axis=1, keepdims=True)
        lse = m + jnp.log(tot)
        probs, dprobs = [], []
        delta = jnp.zeros_like(m)
        for d in range(3):
            p = jnp.exp(scores[d] - lse)
            dp = lax.dot_general(gj, vals[d], NT, preferred_element_type=jnp.float32)
            delta = delta + jnp.sum(p * dp, axis=1, keepdims=True)
            probs.append(p)
            dprobs.append(dp)
        dq = jnp.zeros((tok, HEAD_SIZE), jnp.float32)
        for d in range(3):
            ds = (probs[d] * (dprobs[d] - delta)).astype(jnp.bfloat16)
            ph = probs[d].astype(jnp.bfloat16)
            dq = dq + jnp.dot(ds, keys[d], preferred_element_type=jnp.float32)
            dk[d] = dk[d] + lax.dot_general(ds, qj, TN, preferred_element_type=jnp.float32)
            dv[d] = dv[d] + lax.dot_general(ph, gj, TN, preferred_element_type=jnp.float32)
        dq_ref[:, j * HEAD_SIZE:(j + 1) * HEAD_SIZE] = score_scale * dq
    for d in range(3):
        dkv_refs[d][0] = score_scale * dk[d]
        dkv_refs[d][1] = dv[d]


def attend(rel, x_all, kv_blocks):
    tok = x_all.shape[0]
    kvcols = kv_blocks[0].shape[1] // 2
    groups = kvcols // HEAD_SIZE
    qblk = 2 * kvcols // groups
    col = lambda off: pl.BlockSpec((tok, HEAD_SIZE), lambda g: (0, off + g))
    qcol = lambda off: pl.BlockSpec((tok, qblk), lambda g: (0, off + g))
    kv_spec = pl.BlockSpec((2, tok, HEAD_SIZE), lambda g: (0, 0, g))
    return pl.pallas_call(
        attn_kernel,
        grid=(groups,),
        in_specs=[
            pl.BlockSpec((tok, 1), lambda g: (0, 0)),
            qcol(2 * kvcols // qblk),
            qcol(4 * kvcols // qblk),
            col(0),
            col(groups),
            col(0),
            col(groups),
            col(0),
            col(groups),
        ],
        out_specs=[pl.BlockSpec((tok, qblk), lambda g: (0, g)), kv_spec, kv_spec, kv_spec],
        out_shape=[
            jax.ShapeDtypeStruct((tok, 2 * kvcols), jnp.float32),
            jax.ShapeDtypeStruct((2, tok, kvcols), jnp.float32),
            jax.ShapeDtypeStruct((2, tok, kvcols), jnp.float32),
            jax.ShapeDtypeStruct((2, tok, kvcols), jnp.float32),
        ],
    )(rel, x_all, x_all, x_all, x_all, kv_blocks[0], kv_blocks[0], kv_blocks[1], kv_blocks[1])


def passed_along(block, axis, distance):
    devices = range(lax.axis_size(axis))
    route = [(i - distance, i) for i in devices if i - distance in devices]
    return lax.ppermute(block, axis, route)


def chunk_pass(x_in, rel, kv_cols, q_cols):
    tok_rows = rel.shape[0]
    x_all = lax.all_to_all(x_in, "head", split_axis=1, concat_axis=0, tiled=True)
    x_all = x_all.reshape(tok_rows, 2 * kv_cols + 2 * q_cols)
    kv_local = x_all[:, : 2 * kv_cols]
    if CHAIN:
        kv1 = passed_along(kv_local, "ctx", 1)
        kv2 = passed_along(kv1, "ctx", 1)
    else:
        kv1 = passed_along(kv_local, "ctx", 1)
        kv2 = passed_along(kv_local, "ctx", 2)
    dq, dkv0, dkv1, dkv2 = attend(rel, x_all, (kv1, kv2))
    if CHAIN:
        carried = passed_along(dkv2.astype(jnp.bfloat16), "ctx", -1)
        carried = passed_along((dkv1 + carried).astype(jnp.bfloat16), "ctx", -1)
        kv_total = dkv0 + carried
    else:
        kv_total = dkv0
        for distance, part in ((1, dkv1), (2, dkv2)):
            kv_total = kv_total + passed_along(part.astype(jnp.bfloat16), "ctx", -distance)
    out_loc = jnp.concatenate(
        [dq.astype(jnp.bfloat16), kv_total[0].astype(jnp.bfloat16), kv_total[1].astype(jnp.bfloat16)],
        axis=1,
    )[:, None]
    return lax.all_to_all(out_loc, "head", split_axis=0, concat_axis=1, tiled=True)


def local(queries, normed_key_state, value_state_rows, output_gradient, doc_start):
    heads_ax = lax.axis_size("head")
    rows_in = queries.shape[0]
    tok_rows = doc_start.shape[0]
    kv_cols = normed_key_state.shape[1] // (heads_ax * CHUNKS)
    q_cols = queries.shape[1] // (heads_ax * CHUNKS)
    shard_index = lax.axis_index("ctx")
    rel = (doc_start - shard_index * tok_rows).reshape(tok_rows, 1)
    parts = [
        normed_key_state.reshape(rows_in, heads_ax, CHUNKS, kv_cols),
        value_state_rows.reshape(rows_in, heads_ax, CHUNKS, kv_cols),
        queries.reshape(rows_in, heads_ax, CHUNKS, q_cols),
        output_gradient.reshape(rows_in, heads_ax, CHUNKS, q_cols),
    ]
    outs = []
    for chunk in range(CHUNKS):
        x_in = jnp.concatenate([p[:, :, chunk] for p in parts], axis=2)
        outs.append(chunk_pass(x_in, rel, kv_cols, q_cols))
    out = jnp.stack(outs, axis=2)
    grad_q = out[..., :q_cols].reshape(rows_in, heads_ax * CHUNKS * q_cols)
    grad_k = out[..., q_cols : q_cols + kv_cols].reshape(rows_in, heads_ax * CHUNKS * kv_cols)
    grad_v = out[..., q_cols + kv_cols :].reshape(rows_in, heads_ax * CHUNKS * kv_cols)
    return grad_q, grad_k, grad_v


def solution(mesh):
    placed = (
        P(("ctx", "head"), None),
        P(("ctx", "head"), None),
        P(("ctx", "head"), None),
        P(("ctx", "head"), None),
        P("ctx"),
    )
    return jax.shard_map(
        local,
        mesh=mesh,
        in_specs=placed,
        out_specs=(P(("ctx", "head"), None), P(("ctx", "head"), None), P(("ctx", "head"), None)),
        check_vma=False,
    )
```

```python
import jax
import jax.numpy as jnp
from jax import lax
from jax.experimental import pallas as pl
from jax.sharding import PartitionSpec as P

QUERY_HEADS = 32
KEY_VALUE_HEADS = 16
HEAD_SIZE = 128
WINDOW = 512
SPAN = 2
CHAIN = True
CHUNKS = 2

score_scale = 168.0 ** (-0.5)
NT = (((1,), (1,)), ((), ()))
TN = (((0,), (0,)), ((), ()))


def attn_kernel(rel_ref, q_ref, g_ref, k0_ref, v0_ref, k1_ref, v1_ref, k2_ref, v2_ref, dq_ref, dkv0_ref, dkv1_ref, dkv2_ref):
    tok = q_ref.shape[0]
    dkv_refs = (dkv0_ref, dkv1_ref, dkv2_ref)
    share = q_ref.shape[1] // HEAD_SIZE
    row = lax.broadcasted_iota(jnp.int32, (tok, tok), 0)
    col = lax.broadcasted_iota(jnp.int32, (tok, tok), 1)
    rel = rel_ref[...]
    masks = []
    for d in range(3):
        key_rel = col - tok * d
        masks.append((key_rel >= rel) & (key_rel <= row) & (row - key_rel < WINDOW))
    keys = [k0_ref[...], k1_ref[...], k2_ref[...]]
    vals = [v0_ref[...], v1_ref[...], v2_ref[...]]
    dk = [jnp.zeros((tok, HEAD_SIZE), jnp.float32) for _ in range(3)]
    dv = [jnp.zeros((tok, HEAD_SIZE), jnp.float32) for _ in range(3)]
    for j in range(share):
        qj = q_ref[:, j * HEAD_SIZE:(j + 1) * HEAD_SIZE]
        gj = g_ref[:, j * HEAD_SIZE:(j + 1) * HEAD_SIZE]
        scores = []
        for d in range(3):
            s = score_scale * lax.dot_general(qj, keys[d], NT, preferred_element_type=jnp.float32)
            scores.append(jnp.where(masks[d], s, -jnp.inf))
        m = jnp.max(scores[0], axis=1, keepdims=True)
        for d in range(1, 3):
            m = jnp.maximum(m, jnp.max(scores[d], axis=1, keepdims=True))
        tot = jnp.zeros_like(m)
        for d in range(3):
            tot = tot + jnp.sum(jnp.exp(scores[d] - m), axis=1, keepdims=True)
        lse = m + jnp.log(tot)
        probs, dprobs = [], []
        delta = jnp.zeros_like(m)
        for d in range(3):
            p = jnp.exp(scores[d] - lse)
            dp = lax.dot_general(gj, vals[d], NT, preferred_element_type=jnp.float32)
            delta = delta + jnp.sum(p * dp, axis=1, keepdims=True)
            probs.append(p)
            dprobs.append(dp)
        dq = jnp.zeros((tok, HEAD_SIZE), jnp.float32)
        for d in range(3):
            ds = (probs[d] * (dprobs[d] - delta)).astype(jnp.bfloat16)
            ph = probs[d].astype(jnp.bfloat16)
            dq = dq + jnp.dot(ds, keys[d], preferred_element_type=jnp.float32)
            dk[d] = dk[d] + lax.dot_general(ds, qj, TN, preferred_element_type=jnp.float32)
            dv[d] = dv[d] + lax.dot_general(ph, gj, TN, preferred_element_type=jnp.float32)
        dq_ref[:, j * HEAD_SIZE:(j + 1) * HEAD_SIZE] = score_scale * dq
    for d in range(3):
        dkv_refs[d][0] = score_scale * dk[d]
        dkv_refs[d][1] = dv[d]


def attend(rel, x_all, kv_blocks):
    tok = x_all.shape[0]
    kvcols = kv_blocks[0].shape[1] // 2
    groups = kvcols // HEAD_SIZE
    qblk = 2 * kvcols // groups
    col = lambda off: pl.BlockSpec((tok, HEAD_SIZE), lambda g: (0, off + g))
    qcol = lambda off: pl.BlockSpec((tok, qblk), lambda g: (0, off + g))
    kv_spec = pl.BlockSpec((2, tok, HEAD_SIZE), lambda g: (0, 0, g))
    return pl.pallas_call(
        attn_kernel,
        grid=(groups,),
        in_specs=[
            pl.BlockSpec((tok, 1), lambda g: (0, 0)),
            qcol(2 * kvcols // qblk),
            qcol(4 * kvcols // qblk),
            col(0),
            col(groups),
            col(0),
            col(groups),
            col(0),
            col(groups),
        ],
        out_specs=[pl.BlockSpec((tok, qblk), lambda g: (0, g)), kv_spec, kv_spec, kv_spec],
        out_shape=[
            jax.ShapeDtypeStruct((tok, 2 * kvcols), jnp.float32),
            jax.ShapeDtypeStruct((2, tok, kvcols), jnp.float32),
            jax.ShapeDtypeStruct((2, tok, kvcols), jnp.float32),
            jax.ShapeDtypeStruct((2, tok, kvcols), jnp.float32),
        ],
    )(rel, x_all, x_all, x_all, x_all, kv_blocks[0], kv_blocks[0], kv_blocks[1], kv_blocks[1])


def passed_along(block, axis, distance):
    devices = range(lax.axis_size(axis))
    route = [(i - distance, i) for i in devices if i - distance in devices]
    return lax.ppermute(block, axis, route)


def chunk_pass(x_in, rel, kv_cols, q_cols):
    tok_rows = rel.shape[0]
    x_all = lax.all_to_all(x_in, "head", split_axis=1, concat_axis=0, tiled=True)
    x_all = x_all.reshape(tok_rows, 2 * kv_cols + 2 * q_cols)
    kv_local = x_all[:, : 2 * kv_cols]
    if CHAIN:
        kv1 = passed_along(kv_local, "ctx", 1)
        kv2 = passed_along(kv1, "ctx", 1)
    else:
        kv1 = passed_along(kv_local, "ctx", 1)
        kv2 = passed_along(kv_local, "ctx", 2)
    dq, dkv0, dkv1, dkv2 = attend(rel, x_all, (kv1, kv2))
    if CHAIN:
        carried = passed_along(dkv2.astype(jnp.bfloat16), "ctx", -1)
        carried = passed_along((dkv1 + carried).astype(jnp.bfloat16), "ctx", -1)
        kv_total = dkv0 + carried
    else:
        kv_total = dkv0
        for distance, part in ((1, dkv1), (2, dkv2)):
            kv_total = kv_total + passed_along(part.astype(jnp.bfloat16), "ctx", -distance)
    out_loc = jnp.concatenate(
        [dq.astype(jnp.bfloat16), kv_total[0].astype(jnp.bfloat16), kv_total[1].astype(jnp.bfloat16)],
        axis=1,
    )[:, None]
    return lax.all_to_all(out_loc, "head", split_axis=0, concat_axis=1, tiled=True)


def local(queries, normed_key_state, value_state_rows, output_gradient, doc_start):
    heads_ax = lax.axis_size("head")
    rows_in = queries.shape[0]
    tok_rows = doc_start.shape[0]
    kv_cols = normed_key_state.shape[1] // (heads_ax * CHUNKS)
    q_cols = queries.shape[1] // (heads_ax * CHUNKS)
    shard_index = lax.axis_index("ctx")
    rel = (doc_start - shard_index * tok_rows).reshape(tok_rows, 1)
    parts = [
        normed_key_state.reshape(rows_in, heads_ax, CHUNKS, kv_cols),
        value_state_rows.reshape(rows_in, heads_ax, CHUNKS, kv_cols),
        queries.reshape(rows_in, heads_ax, CHUNKS, q_cols),
        output_gradient.reshape(rows_in, heads_ax, CHUNKS, q_cols),
    ]
    outs = []
    for chunk in range(CHUNKS):
        x_in = jnp.concatenate([p[:, :, chunk] for p in parts], axis=2)
        outs.append(chunk_pass(x_in, rel, kv_cols, q_cols))
    out = jnp.stack(outs, axis=2)
    grad_q = out[..., :q_cols].reshape(rows_in, heads_ax * CHUNKS * q_cols)
    grad_k = out[..., q_cols : q_cols + kv_cols].reshape(rows_in, heads_ax * CHUNKS * kv_cols)
    grad_v = out[..., q_cols + kv_cols :].reshape(rows_in, heads_ax * CHUNKS * kv_cols)
    return grad_q, grad_k, grad_v


def solution(mesh):
    placed = (
        P(("ctx", "head"), None),
        P(("ctx", "head"), None),
        P(("ctx", "head"), None),
        P(("ctx", "head"), None),
        P("ctx"),
    )
    return jax.shard_map(
        local,
        mesh=mesh,
        in_specs=placed,
        out_specs=(P(("ctx", "head"), None), P(("ctx", "head"), None), P(("ctx", "head"), None)),
        check_vma=False,
    )
```

```python
import jax
import jax.numpy as jnp
from jax import lax
from jax.experimental import pallas as pl
from jax.sharding import PartitionSpec as P

QUERY_HEADS = 32
KEY_VALUE_HEADS = 16
HEAD_SIZE = 128
WINDOW = 512
SPAN = 2
CHAIN = False
CHUNKS = 4

score_scale = 168.0 ** (-0.5)
NT = (((1,), (1,)), ((), ()))
TN = (((0,), (0,)), ((), ()))


def attn_kernel(rel_ref, q_ref, g_ref, k0_ref, v0_ref, k1_ref, v1_ref, k2_ref, v2_ref, dq_ref, dkv0_ref, dkv1_ref, dkv2_ref):
    tok = q_ref.shape[0]
    dkv_refs = (dkv0_ref, dkv1_ref, dkv2_ref)
    share = q_ref.shape[1] // HEAD_SIZE
    row = lax.broadcasted_iota(jnp.int32, (tok, tok), 0)
    col = lax.broadcasted_iota(jnp.int32, (tok, tok), 1)
    rel = rel_ref[...]
    masks = []
    for d in range(3):
        key_rel = col - tok * d
        masks.append((key_rel >= rel) & (key_rel <= row) & (row - key_rel < WINDOW))
    keys = [k0_ref[...], k1_ref[...], k2_ref[...]]
    vals = [v0_ref[...], v1_ref[...], v2_ref[...]]
    dk = [jnp.zeros((tok, HEAD_SIZE), jnp.float32) for _ in range(3)]
    dv = [jnp.zeros((tok, HEAD_SIZE), jnp.float32) for _ in range(3)]
    for j in range(share):
        qj = q_ref[:, j * HEAD_SIZE:(j + 1) * HEAD_SIZE]
        gj = g_ref[:, j * HEAD_SIZE:(j + 1) * HEAD_SIZE]
        scores = []
        for d in range(3):
            s = score_scale * lax.dot_general(qj, keys[d], NT, preferred_element_type=jnp.float32)
            scores.append(jnp.where(masks[d], s, -jnp.inf))
        m = jnp.max(scores[0], axis=1, keepdims=True)
        for d in range(1, 3):
            m = jnp.maximum(m, jnp.max(scores[d], axis=1, keepdims=True))
        tot = jnp.zeros_like(m)
        for d in range(3):
            tot = tot + jnp.sum(jnp.exp(scores[d] - m), axis=1, keepdims=True)
        lse = m + jnp.log(tot)
        probs, dprobs = [], []
        delta = jnp.zeros_like(m)
        for d in range(3):
            p = jnp.exp(scores[d] - lse)
            dp = lax.dot_general(gj, vals[d], NT, preferred_element_type=jnp.float32)
            delta = delta + jnp.sum(p * dp, axis=1, keepdims=True)
            probs.append(p)
            dprobs.append(dp)
        dq = jnp.zeros((tok, HEAD_SIZE), jnp.float32)
        for d in range(3):
            ds = (probs[d] * (dprobs[d] - delta)).astype(jnp.bfloat16)
            ph = probs[d].astype(jnp.bfloat16)
            dq = dq + jnp.dot(ds, keys[d], preferred_element_type=jnp.float32)
            dk[d] = dk[d] + lax.dot_general(ds, qj, TN, preferred_element_type=jnp.float32)
            dv[d] = dv[d] + lax.dot_general(ph, gj, TN, preferred_element_type=jnp.float32)
        dq_ref[:, j * HEAD_SIZE:(j + 1) * HEAD_SIZE] = score_scale * dq
    for d in range(3):
        dkv_refs[d][0] = score_scale * dk[d]
        dkv_refs[d][1] = dv[d]


def attend(rel, x_all, kv_blocks):
    tok = x_all.shape[0]
    kvcols = kv_blocks[0].shape[1] // 2
    groups = kvcols // HEAD_SIZE
    qblk = 2 * kvcols // groups
    col = lambda off: pl.BlockSpec((tok, HEAD_SIZE), lambda g: (0, off + g))
    qcol = lambda off: pl.BlockSpec((tok, qblk), lambda g: (0, off + g))
    kv_spec = pl.BlockSpec((2, tok, HEAD_SIZE), lambda g: (0, 0, g))
    return pl.pallas_call(
        attn_kernel,
        grid=(groups,),
        in_specs=[
            pl.BlockSpec((tok, 1), lambda g: (0, 0)),
            qcol(2 * kvcols // qblk),
            qcol(4 * kvcols // qblk),
            col(0),
            col(groups),
            col(0),
            col(groups),
            col(0),
            col(groups),
        ],
        out_specs=[pl.BlockSpec((tok, qblk), lambda g: (0, g)), kv_spec, kv_spec, kv_spec],
        out_shape=[
            jax.ShapeDtypeStruct((tok, 2 * kvcols), jnp.float32),
            jax.ShapeDtypeStruct((2, tok, kvcols), jnp.float32),
            jax.ShapeDtypeStruct((2, tok, kvcols), jnp.float32),
            jax.ShapeDtypeStruct((2, tok, kvcols), jnp.float32),
        ],
    )(rel, x_all, x_all, x_all, x_all, kv_blocks[0], kv_blocks[0], kv_blocks[1], kv_blocks[1])


def passed_along(block, axis, distance):
    devices = range(lax.axis_size(axis))
    route = [(i - distance, i) for i in devices if i - distance in devices]
    return lax.ppermute(block, axis, route)


def chunk_pass(x_in, rel, kv_cols, q_cols):
    tok_rows = rel.shape[0]
    x_all = lax.all_to_all(x_in, "head", split_axis=1, concat_axis=0, tiled=True)
    x_all = x_all.reshape(tok_rows, 2 * kv_cols + 2 * q_cols)
    kv_local = x_all[:, : 2 * kv_cols]
    if CHAIN:
        kv1 = passed_along(kv_local, "ctx", 1)
        kv2 = passed_along(kv1, "ctx", 1)
    else:
        kv1 = passed_along(kv_local, "ctx", 1)
        kv2 = passed_along(kv_local, "ctx", 2)
    dq, dkv0, dkv1, dkv2 = attend(rel, x_all, (kv1, kv2))
    if CHAIN:
        carried = passed_along(dkv2.astype(jnp.bfloat16), "ctx", -1)
        carried = passed_along((dkv1 + carried).astype(jnp.bfloat16), "ctx", -1)
        kv_total = dkv0 + carried
    else:
        kv_total = dkv0
        for distance, part in ((1, dkv1), (2, dkv2)):
            kv_total = kv_total + passed_along(part.astype(jnp.bfloat16), "ctx", -distance)
    out_loc = jnp.concatenate(
        [dq.astype(jnp.bfloat16), kv_total[0].astype(jnp.bfloat16), kv_total[1].astype(jnp.bfloat16)],
        axis=1,
    )[:, None]
    return lax.all_to_all(out_loc, "head", split_axis=0, concat_axis=1, tiled=True)


def local(queries, normed_key_state, value_state_rows, output_gradient, doc_start):
    heads_ax = lax.axis_size("head")
    rows_in = queries.shape[0]
    tok_rows = doc_start.shape[0]
    kv_cols = normed_key_state.shape[1] // (heads_ax * CHUNKS)
    q_cols = queries.shape[1] // (heads_ax * CHUNKS)
    shard_index = lax.axis_index("ctx")
    rel = (doc_start - shard_index * tok_rows).reshape(tok_rows, 1)
    parts = [
        normed_key_state.reshape(rows_in, heads_ax, CHUNKS, kv_cols),
        value_state_rows.reshape(rows_in, heads_ax, CHUNKS, kv_cols),
        queries.reshape(rows_in, heads_ax, CHUNKS, q_cols),
        output_gradient.reshape(rows_in, heads_ax, CHUNKS, q_cols),
    ]
    outs = []
    for chunk in range(CHUNKS):
        x_in = jnp.concatenate([p[:, :, chunk] for p in parts], axis=2)
        outs.append(chunk_pass(x_in, rel, kv_cols, q_cols))
    out = jnp.stack(outs, axis=2)
    grad_q = out[..., :q_cols].reshape(rows_in, heads_ax * CHUNKS * q_cols)
    grad_k = out[..., q_cols : q_cols + kv_cols].reshape(rows_in, heads_ax * CHUNKS * kv_cols)
    grad_v = out[..., q_cols + kv_cols :].reshape(rows_in, heads_ax * CHUNKS * kv_cols)
    return grad_q, grad_k, grad_v


def solution(mesh):
    placed = (
        P(("ctx", "head"), None),
        P(("ctx", "head"), None),
        P(("ctx", "head"), None),
        P(("ctx", "head"), None),
        P("ctx"),
    )
    return jax.shard_map(
        local,
        mesh=mesh,
        in_specs=placed,
        out_specs=(P(("ctx", "head"), None), P(("ctx", "head"), None), P(("ctx", "head"), None)),
        check_vma=False,
    )
```

```python
import jax
import jax.numpy as jnp
from jax import lax
from jax.experimental import pallas as pl
from jax.sharding import PartitionSpec as P

QUERY_HEADS = 32
KEY_VALUE_HEADS = 16
HEAD_SIZE = 128
WINDOW = 512
SPAN = 2
CHAIN = False
CHUNKS = 2

score_scale = 168.0 ** (-0.5)
NT = (((1,), (1,)), ((), ()))
TN = (((0,), (0,)), ((), ()))


def attn_kernel(rel_ref, q_ref, g_ref, k0_ref, v0_ref, k1_ref, v1_ref, k2_ref, v2_ref, dq_ref, dkv0_ref, dkv1_ref, dkv2_ref):
    tok = q_ref.shape[0]
    dkv_refs = (dkv0_ref, dkv1_ref, dkv2_ref)
    share = q_ref.shape[1] // HEAD_SIZE
    row = lax.broadcasted_iota(jnp.int32, (tok, tok), 0)
    col = lax.broadcasted_iota(jnp.int32, (tok, tok), 1)
    rel = rel_ref[...]
    masks = []
    for d in range(3):
        key_rel = col - tok * d
        masks.append((key_rel >= rel) & (key_rel <= row) & (row - key_rel < WINDOW))
    keys = [k0_ref[...], k1_ref[...], k2_ref[...]]
    vals = [v0_ref[...], v1_ref[...], v2_ref[...]]
    dk = [jnp.zeros((tok, HEAD_SIZE), jnp.float32) for _ in range(3)]
    dv = [jnp.zeros((tok, HEAD_SIZE), jnp.float32) for _ in range(3)]
    for j in range(share):
        qj = q_ref[:, j * HEAD_SIZE:(j + 1) * HEAD_SIZE]
        gj = g_ref[:, j * HEAD_SIZE:(j + 1) * HEAD_SIZE]
        scores = []
        for d in range(3):
            s = score_scale * lax.dot_general(qj, keys[d], NT, preferred_element_type=jnp.float32)
            scores.append(jnp.where(masks[d], s, -jnp.inf))
        m = jnp.max(scores[0], axis=1, keepdims=True)
        for d in range(1, 3):
            m = jnp.maximum(m, jnp.max(scores[d], axis=1, keepdims=True))
        weights = [jnp.exp(scores[d] - m) for d in range(3)]
        tot = jnp.zeros_like(m)
        for d in range(3):
            tot = tot + jnp.sum(weights[d], axis=1, keepdims=True)
        inv_tot = 1.0 / tot
        probs, dprobs = [], []
        delta = jnp.zeros_like(m)
        for d in range(3):
            p = weights[d] * inv_tot
            dp = lax.dot_general(gj, vals[d], NT, preferred_element_type=jnp.float32)
            delta = delta + jnp.sum(p * dp, axis=1, keepdims=True)
            probs.append(p)
            dprobs.append(dp)
        dq = jnp.zeros((tok, HEAD_SIZE), jnp.float32)
        for d in range(3):
            ds = (probs[d] * (dprobs[d] - delta)).astype(jnp.bfloat16)
            ph = probs[d].astype(jnp.bfloat16)
            dq = dq + jnp.dot(ds, keys[d], preferred_element_type=jnp.float32)
            dk[d] = dk[d] + lax.dot_general(ds, qj, TN, preferred_element_type=jnp.float32)
            dv[d] = dv[d] + lax.dot_general(ph, gj, TN, preferred_element_type=jnp.float32)
        dq_ref[:, j * HEAD_SIZE:(j + 1) * HEAD_SIZE] = score_scale * dq
    for d in range(3):
        dkv_refs[d][0] = score_scale * dk[d]
        dkv_refs[d][1] = dv[d]


def attend(rel, x_all, kv_blocks):
    tok = x_all.shape[0]
    kvcols = kv_blocks[0].shape[1] // 2
    groups = kvcols // HEAD_SIZE
    qblk = 2 * kvcols // groups
    col = lambda off: pl.BlockSpec((tok, HEAD_SIZE), lambda g: (0, off + g))
    qcol = lambda off: pl.BlockSpec((tok, qblk), lambda g: (0, off + g))
    kv_spec = pl.BlockSpec((2, tok, HEAD_SIZE), lambda g: (0, 0, g))
    return pl.pallas_call(
        attn_kernel,
        grid=(groups,),
        in_specs=[
            pl.BlockSpec((tok, 1), lambda g: (0, 0)),
            qcol(2 * kvcols // qblk),
            qcol(4 * kvcols // qblk),
            col(0),
            col(groups),
            col(0),
            col(groups),
            col(0),
            col(groups),
        ],
        out_specs=[pl.BlockSpec((tok, qblk), lambda g: (0, g)), kv_spec, kv_spec, kv_spec],
        out_shape=[
            jax.ShapeDtypeStruct((tok, 2 * kvcols), jnp.float32),
            jax.ShapeDtypeStruct((2, tok, kvcols), jnp.float32),
            jax.ShapeDtypeStruct((2, tok, kvcols), jnp.float32),
            jax.ShapeDtypeStruct((2, tok, kvcols), jnp.float32),
        ],
    )(rel, x_all, x_all, x_all, x_all, kv_blocks[0], kv_blocks[0], kv_blocks[1], kv_blocks[1])


def passed_along(block, axis, distance):
    devices = range(lax.axis_size(axis))
    route = [(i - distance, i) for i in devices if i - distance in devices]
    return lax.ppermute(block, axis, route)


def chunk_pass(x_in, rel, kv_cols, q_cols):
    tok_rows = rel.shape[0]
    x_all = lax.all_to_all(x_in, "head", split_axis=1, concat_axis=0, tiled=True)
    x_all = x_all.reshape(tok_rows, 2 * kv_cols + 2 * q_cols)
    kv_local = x_all[:, : 2 * kv_cols]
    if CHAIN:
        kv1 = passed_along(kv_local, "ctx", 1)
        kv2 = passed_along(kv1, "ctx", 1)
    else:
        kv1 = passed_along(kv_local, "ctx", 1)
        kv2 = passed_along(kv_local, "ctx", 2)
    dq, dkv0, dkv1, dkv2 = attend(rel, x_all, (kv1, kv2))
    if CHAIN:
        carried = passed_along(dkv2.astype(jnp.bfloat16), "ctx", -1)
        carried = passed_along((dkv1 + carried).astype(jnp.bfloat16), "ctx", -1)
        kv_total = dkv0 + carried
    else:
        kv_total = dkv0
        for distance, part in ((1, dkv1), (2, dkv2)):
            kv_total = kv_total + passed_along(part.astype(jnp.bfloat16), "ctx", -distance)
    return jnp.concatenate(
        [dq.astype(jnp.bfloat16), kv_total[0].astype(jnp.bfloat16), kv_total[1].astype(jnp.bfloat16)],
        axis=1,
    )


def local(queries, normed_key_state, value_state_rows, output_gradient, doc_start):
    heads_ax = lax.axis_size("head")
    rows_in = queries.shape[0]
    tok_rows = doc_start.shape[0]
    kv_cols = normed_key_state.shape[1] // (heads_ax * CHUNKS)
    q_cols = queries.shape[1] // (heads_ax * CHUNKS)
    shard_index = lax.axis_index("ctx")
    rel = (doc_start - shard_index * tok_rows).reshape(tok_rows, 1)
    parts = [
        normed_key_state.reshape(rows_in, heads_ax, CHUNKS, kv_cols),
        value_state_rows.reshape(rows_in, heads_ax, CHUNKS, kv_cols),
        queries.reshape(rows_in, heads_ax, CHUNKS, q_cols),
        output_gradient.reshape(rows_in, heads_ax, CHUNKS, q_cols),
    ]
    outs = []
    for chunk in range(CHUNKS):
        x_in = jnp.concatenate([p[:, :, chunk] for p in parts], axis=2)
        outs.append(chunk_pass(x_in, rel, kv_cols, q_cols))
    out_loc = jnp.stack(outs, axis=1)[:, None]
    out = lax.all_to_all(out_loc, "head", split_axis=0, concat_axis=1, tiled=True)
    grad_q = out[..., :q_cols].reshape(rows_in, heads_ax * CHUNKS * q_cols)
    grad_k = out[..., q_cols : q_cols + kv_cols].reshape(rows_in, heads_ax * CHUNKS * kv_cols)
    grad_v = out[..., q_cols + kv_cols :].reshape(rows_in, heads_ax * CHUNKS * kv_cols)
    return grad_q, grad_k, grad_v


def solution(mesh):
    placed = (
        P(("ctx", "head"), None),
        P(("ctx", "head"), None),
        P(("ctx", "head"), None),
        P(("ctx", "head"), None),
        P("ctx"),
    )
    return jax.shard_map(
        local,
        mesh=mesh,
        in_specs=placed,
        out_specs=(P(("ctx", "head"), None), P(("ctx", "head"), None), P(("ctx", "head"), None)),
        check_vma=False,
    )
```

```python
import jax
import jax.numpy as jnp
from jax import lax
from jax.experimental import pallas as pl
from jax.sharding import PartitionSpec as P

QUERY_HEADS = 32
KEY_VALUE_HEADS = 16
HEAD_SIZE = 128
WINDOW = 512
SPAN = 2
CHAIN = False
CHUNKS = 2

score_scale = 168.0 ** (-0.5)
NT = (((1,), (1,)), ((), ()))
TN = (((0,), (0,)), ((), ()))


def attn_kernel(rel_ref, q_ref, g_ref, k0_ref, v0_ref, k1_ref, v1_ref, k2_ref, v2_ref, dq_ref, dkv0_ref, dkv1_ref, dkv2_ref):
    tok = q_ref.shape[0]
    dkv_refs = (dkv0_ref, dkv1_ref, dkv2_ref)
    share = q_ref.shape[1] // HEAD_SIZE
    row = lax.broadcasted_iota(jnp.int32, (tok, tok), 0)
    col = lax.broadcasted_iota(jnp.int32, (tok, tok), 1)
    rel = rel_ref[...]
    masks = []
    for d in range(3):
        key_rel = col - tok * d
        masks.append((key_rel >= rel) & (key_rel <= row) & (row - key_rel < WINDOW))
    keys = [k0_ref[...], k1_ref[...], k2_ref[...]]
    vals = [v0_ref[...], v1_ref[...], v2_ref[...]]
    dk = [jnp.zeros((tok, HEAD_SIZE), jnp.float32) for _ in range(3)]
    dv = [jnp.zeros((tok, HEAD_SIZE), jnp.float32) for _ in range(3)]
    for j in range(share):
        qj = q_ref[:, j * HEAD_SIZE:(j + 1) * HEAD_SIZE]
        gj = g_ref[:, j * HEAD_SIZE:(j + 1) * HEAD_SIZE]
        scores = []
        for d in range(3):
            s = score_scale * lax.dot_general(qj, keys[d], NT, preferred_element_type=jnp.float32)
            scores.append(jnp.where(masks[d], s, -jnp.inf))
        m = jnp.max(scores[0], axis=1, keepdims=True)
        for d in range(1, 3):
            m = jnp.maximum(m, jnp.max(scores[d], axis=1, keepdims=True))
        weights = [jnp.exp(scores[d] - m) for d in range(3)]
        tot = jnp.zeros_like(m)
        for d in range(3):
            tot = tot + jnp.sum(weights[d], axis=1, keepdims=True)
        inv_tot = 1.0 / tot
        probs, dprobs = [], []
        delta = jnp.zeros_like(m)
        for d in range(3):
            p = weights[d] * inv_tot
            dp = lax.dot_general(gj, vals[d], NT, preferred_element_type=jnp.float32)
            delta = delta + jnp.sum(p * dp, axis=1, keepdims=True)
            probs.append(p)
            dprobs.append(dp)
        dq = jnp.zeros((tok, HEAD_SIZE), jnp.float32)
        for d in range(3):
            ds = (probs[d] * (dprobs[d] - delta)).astype(jnp.bfloat16)
            ph = probs[d].astype(jnp.bfloat16)
            dq = dq + jnp.dot(ds, keys[d], preferred_element_type=jnp.float32)
            dk[d] = dk[d] + lax.dot_general(ds, qj, TN, preferred_element_type=jnp.float32)
            dv[d] = dv[d] + lax.dot_general(ph, gj, TN, preferred_element_type=jnp.float32)
        dq_ref[:, j * HEAD_SIZE:(j + 1) * HEAD_SIZE] = score_scale * dq
    for d in range(3):
        dkv_refs[d][0] = score_scale * dk[d]
        dkv_refs[d][1] = dv[d]


def attend(rel, x_all, kv_blocks):
    tok = x_all.shape[0]
    kvcols = kv_blocks[0].shape[1] // 2
    groups = kvcols // HEAD_SIZE
    qblk = 2 * kvcols // groups
    col = lambda off: pl.BlockSpec((tok, HEAD_SIZE), lambda g: (0, off + g))
    qcol = lambda off: pl.BlockSpec((tok, qblk), lambda g: (0, off + g))
    kv_spec = pl.BlockSpec((2, tok, HEAD_SIZE), lambda g: (0, 0, g))
    return pl.pallas_call(
        attn_kernel,
        grid=(groups,),
        in_specs=[
            pl.BlockSpec((tok, 1), lambda g: (0, 0)),
            qcol(2 * kvcols // qblk),
            qcol(4 * kvcols // qblk),
            col(0),
            col(groups),
            col(0),
            col(groups),
            col(0),
            col(groups),
        ],
        out_specs=[pl.BlockSpec((tok, qblk), lambda g: (0, g)), kv_spec, kv_spec, kv_spec],
        out_shape=[
            jax.ShapeDtypeStruct((tok, 2 * kvcols), jnp.float32),
            jax.ShapeDtypeStruct((2, tok, kvcols), jnp.float32),
            jax.ShapeDtypeStruct((2, tok, kvcols), jnp.float32),
            jax.ShapeDtypeStruct((2, tok, kvcols), jnp.float32),
        ],
    )(rel, x_all, x_all, x_all, x_all, kv_blocks[0], kv_blocks[0], kv_blocks[1], kv_blocks[1])


def passed_along(block, axis, distance):
    devices = range(lax.axis_size(axis))
    route = [(i - distance, i) for i in devices if i - distance in devices]
    return lax.ppermute(block, axis, route)


def chunk_pass(x_in, rel, kv_cols, q_cols):
    tok_rows = rel.shape[0]
    x_all = lax.all_to_all(x_in, "head", split_axis=1, concat_axis=0, tiled=True)
    x_all = x_all.reshape(tok_rows, 2 * kv_cols + 2 * q_cols)
    kv_local = x_all[:, : 2 * kv_cols]
    if CHAIN:
        kv1 = passed_along(kv_local, "ctx", 1)
        kv2 = passed_along(kv1, "ctx", 1)
    else:
        kv1 = passed_along(kv_local, "ctx", 1)
        kv2 = passed_along(kv_local, "ctx", 2)
    dq, dkv0, dkv1, dkv2 = attend(rel, x_all, (kv1, kv2))
    if CHAIN:
        carried = passed_along(dkv2.astype(jnp.bfloat16), "ctx", -1)
        carried = passed_along((dkv1 + carried).astype(jnp.bfloat16), "ctx", -1)
        kv_total = dkv0 + carried
    else:
        kv_total = dkv0
        for distance, part in ((1, dkv1), (2, dkv2)):
            kv_total = kv_total + passed_along(part.astype(jnp.bfloat16), "ctx", -distance)
    out_loc = jnp.concatenate(
        [dq.astype(jnp.bfloat16), kv_total[0].astype(jnp.bfloat16), kv_total[1].astype(jnp.bfloat16)],
        axis=1,
    )[:, None]
    return lax.all_to_all(out_loc, "head", split_axis=0, concat_axis=1, tiled=True)


def local(queries, normed_key_state, value_state_rows, output_gradient, doc_start):
    heads_ax = lax.axis_size("head")
    rows_in = queries.shape[0]
    tok_rows = doc_start.shape[0]
    kv_cols = normed_key_state.shape[1] // (heads_ax * CHUNKS)
    q_cols = queries.shape[1] // (heads_ax * CHUNKS)
    shard_index = lax.axis_index("ctx")
    rel = (doc_start - shard_index * tok_rows).reshape(tok_rows, 1)
    parts = [
        normed_key_state.reshape(rows_in, heads_ax, CHUNKS, kv_cols),
        value_state_rows.reshape(rows_in, heads_ax, CHUNKS, kv_cols),
        queries.reshape(rows_in, heads_ax, CHUNKS, q_cols),
        output_gradient.reshape(rows_in, heads_ax, CHUNKS, q_cols),
    ]
    outs = []
    for chunk in range(CHUNKS):
        x_in = jnp.concatenate([p[:, :, chunk] for p in parts], axis=2)
        outs.append(chunk_pass(x_in, rel, kv_cols, q_cols))
    out = jnp.stack(outs, axis=2)
    grad_q = out[..., :q_cols].reshape(rows_in, heads_ax * CHUNKS * q_cols)
    grad_k = out[..., q_cols : q_cols + kv_cols].reshape(rows_in, heads_ax * CHUNKS * kv_cols)
    grad_v = out[..., q_cols + kv_cols :].reshape(rows_in, heads_ax * CHUNKS * kv_cols)
    return grad_q, grad_k, grad_v


def solution(mesh):
    placed = (
        P(("ctx", "head"), None),
        P(("ctx", "head"), None),
        P(("ctx", "head"), None),
        P(("ctx", "head"), None),
        P("ctx"),
    )
    return jax.shard_map(
        local,
        mesh=mesh,
        in_specs=placed,
        out_specs=(P(("ctx", "head"), None), P(("ctx", "head"), None), P(("ctx", "head"), None)),
        check_vma=False,
    )
```

```python
import jax
import jax.numpy as jnp
from jax import lax
from jax.experimental import pallas as pl
from jax.sharding import PartitionSpec as P

QUERY_HEADS = 32
KEY_VALUE_HEADS = 16
HEAD_SIZE = 128
WINDOW = 512
SPAN = 2
CHAIN = False
CHUNKS = 2

score_scale = 168.0 ** (-0.5)
NT = (((1,), (1,)), ((), ()))
TN = (((0,), (0,)), ((), ()))


def attn_kernel(rel_ref, q_ref, g_ref, k0_ref, v0_ref, k1_ref, v1_ref, k2_ref, v2_ref, dq_ref, dkv0_ref, dkv1_ref, dkv2_ref):
    tok = q_ref.shape[0]
    dkv_refs = (dkv0_ref, dkv1_ref, dkv2_ref)
    share = q_ref.shape[1] // HEAD_SIZE
    row = lax.broadcasted_iota(jnp.int32, (tok, tok), 0)
    col = lax.broadcasted_iota(jnp.int32, (tok, tok), 1)
    rel = rel_ref[...]
    masks = []
    for d in range(3):
        key_rel = col - tok * d
        masks.append((key_rel >= rel) & (key_rel <= row) & (row - key_rel < WINDOW))
    keys = [k0_ref[...], k1_ref[...], k2_ref[...]]
    vals = [v0_ref[...], v1_ref[...], v2_ref[...]]
    dk = [jnp.zeros((tok, HEAD_SIZE), jnp.float32) for _ in range(3)]
    dv = [jnp.zeros((tok, HEAD_SIZE), jnp.float32) for _ in range(3)]
    for j in range(share):
        qj = q_ref[:, j * HEAD_SIZE:(j + 1) * HEAD_SIZE]
        gj = g_ref[:, j * HEAD_SIZE:(j + 1) * HEAD_SIZE]
        scores = []
        for d in range(3):
            s = score_scale * lax.dot_general(qj, keys[d], NT, preferred_element_type=jnp.float32)
            scores.append(jnp.where(masks[d], s, -jnp.inf))
        m = jnp.max(scores[0], axis=1, keepdims=True)
        for d in range(1, 3):
            m = jnp.maximum(m, jnp.max(scores[d], axis=1, keepdims=True))
        weights = [jnp.exp(scores[d] - m) for d in range(3)]
        tot = jnp.zeros_like(m)
        for d in range(3):
            tot = tot + jnp.sum(weights[d], axis=1, keepdims=True)
        inv_tot = 1.0 / tot
        probs, dprobs = [], []
        delta = jnp.zeros_like(m)
        for d in range(3):
            p = weights[d] * inv_tot
            dp = lax.dot_general(gj, vals[d], NT, preferred_element_type=jnp.float32)
            delta = delta + jnp.sum(p * dp, axis=1, keepdims=True)
            probs.append(p)
            dprobs.append(dp)
        dq = jnp.zeros((tok, HEAD_SIZE), jnp.float32)
        for d in range(3):
            ds = (probs[d] * (dprobs[d] - delta)).astype(jnp.bfloat16)
            ph = probs[d].astype(jnp.bfloat16)
            dq = dq + jnp.dot(ds, keys[d], preferred_element_type=jnp.float32)
            dk[d] = dk[d] + lax.dot_general(ds, qj, TN, preferred_element_type=jnp.float32)
            dv[d] = dv[d] + lax.dot_general(ph, gj, TN, preferred_element_type=jnp.float32)
        dq_ref[:, j * HEAD_SIZE:(j + 1) * HEAD_SIZE] = score_scale * dq
    for d in range(3):
        dkv_refs[d][0] = score_scale * dk[d]
        dkv_refs[d][1] = dv[d]


def attend(rel, x_all, kv_blocks, g0, ng):
    tok = x_all.shape[0]
    kvcols = kv_blocks[0].shape[1] // 2
    groups = kvcols // HEAD_SIZE
    qblk = 2 * kvcols // groups
    col = lambda off: pl.BlockSpec((tok, HEAD_SIZE), lambda g: (0, off + g0 + g))
    qcol = lambda off: pl.BlockSpec((tok, qblk), lambda g: (0, off + g0 + g))
    kv_spec = pl.BlockSpec((2, tok, HEAD_SIZE), lambda g: (0, 0, g))
    out_cols = ng * HEAD_SIZE
    return pl.pallas_call(
        attn_kernel,
        grid=(ng,),
        in_specs=[
            pl.BlockSpec((tok, 1), lambda g: (0, 0)),
            qcol(2 * kvcols // qblk),
            qcol(4 * kvcols // qblk),
            col(0),
            col(groups),
            col(0),
            col(groups),
            col(0),
            col(groups),
        ],
        out_specs=[pl.BlockSpec((tok, qblk), lambda g: (0, g)), kv_spec, kv_spec, kv_spec],
        out_shape=[
            jax.ShapeDtypeStruct((tok, 2 * out_cols), jnp.float32),
            jax.ShapeDtypeStruct((2, tok, out_cols), jnp.float32),
            jax.ShapeDtypeStruct((2, tok, out_cols), jnp.float32),
            jax.ShapeDtypeStruct((2, tok, out_cols), jnp.float32),
        ],
    )(rel, x_all, x_all, x_all, x_all, kv_blocks[0], kv_blocks[0], kv_blocks[1], kv_blocks[1])


def passed_along(block, axis, distance):
    devices = range(lax.axis_size(axis))
    route = [(i - distance, i) for i in devices if i - distance in devices]
    return lax.ppermute(block, axis, route)


def local(queries, normed_key_state, value_state_rows, output_gradient, doc_start):
    heads_ax = lax.axis_size("head")
    rows_in = queries.shape[0]
    tok_rows = doc_start.shape[0]
    kv_cols = normed_key_state.shape[1] // heads_ax
    q_cols = queries.shape[1] // heads_ax
    groups = kv_cols // HEAD_SIZE
    shard_index = lax.axis_index("ctx")
    rel = (doc_start - shard_index * tok_rows).reshape(tok_rows, 1)
    x_in = jnp.concatenate(
        [
            normed_key_state.reshape(rows_in, heads_ax, kv_cols),
            value_state_rows.reshape(rows_in, heads_ax, kv_cols),
            queries.reshape(rows_in, heads_ax, q_cols),
            output_gradient.reshape(rows_in, heads_ax, q_cols),
        ],
        axis=2,
    )
    x_all = lax.all_to_all(x_in, "head", split_axis=1, concat_axis=0, tiled=True)
    x_all = x_all.reshape(tok_rows, 2 * kv_cols + 2 * q_cols)
    kv_local = x_all[:, : 2 * kv_cols]
    kv1 = passed_along(kv_local, "ctx", 1)
    kv2 = passed_along(kv_local, "ctx", 2)
    step = groups // CHUNKS
    outs = []
    for chunk in range(CHUNKS):
        dq, dkv0, dkv1, dkv2 = attend(rel, x_all, (kv1, kv2), chunk * step, step)
        kv_total = dkv0
        for distance, part in ((1, dkv1), (2, dkv2)):
            kv_total = kv_total + passed_along(part.astype(jnp.bfloat16), "ctx", -distance)
        out_loc = jnp.concatenate(
            [dq.astype(jnp.bfloat16), kv_total[0].astype(jnp.bfloat16), kv_total[1].astype(jnp.bfloat16)],
            axis=1,
        )[:, None]
        outs.append(lax.all_to_all(out_loc, "head", split_axis=0, concat_axis=1, tiled=True))
    out = jnp.stack(outs, axis=2)
    qc, kc = q_cols // CHUNKS, kv_cols // CHUNKS
    grad_q = out[..., :qc].reshape(rows_in, heads_ax * q_cols)
    grad_k = out[..., qc : qc + kc].reshape(rows_in, heads_ax * kv_cols)
    grad_v = out[..., qc + kc :].reshape(rows_in, heads_ax * kv_cols)
    return grad_q, grad_k, grad_v


def solution(mesh):
    placed = (
        P(("ctx", "head"), None),
        P(("ctx", "head"), None),
        P(("ctx", "head"), None),
        P(("ctx", "head"), None),
        P("ctx"),
    )
    return jax.shard_map(
        local,
        mesh=mesh,
        in_specs=placed,
        out_specs=(P(("ctx", "head"), None), P(("ctx", "head"), None), P(("ctx", "head"), None)),
        check_vma=False,
    )
```

```python
import jax
import jax.numpy as jnp
from jax import lax
from jax.experimental import pallas as pl
from jax.sharding import PartitionSpec as P

QUERY_HEADS = 32
KEY_VALUE_HEADS = 16
HEAD_SIZE = 128
WINDOW = 512
SPAN = 2
CHAIN = False
CHUNKS = 2

score_scale = 168.0 ** (-0.5)
NT = (((1,), (1,)), ((), ()))
TN = (((0,), (0,)), ((), ()))


def attn_kernel(rel_ref, q_ref, g_ref, k0_ref, v0_ref, k1_ref, v1_ref, k2_ref, v2_ref, dq_ref, dkv0_ref, dkv1_ref, dkv2_ref):
    tok = q_ref.shape[0]
    dkv_refs = (dkv0_ref, dkv1_ref, dkv2_ref)
    share = q_ref.shape[1] // HEAD_SIZE
    row = lax.broadcasted_iota(jnp.int32, (tok, tok), 0)
    col = lax.broadcasted_iota(jnp.int32, (tok, tok), 1)
    rel = rel_ref[...]
    masks = []
    for d in range(3):
        key_rel = col - tok * d
        masks.append((key_rel >= rel) & (key_rel <= row) & (row - key_rel < WINDOW))
    keys = [k0_ref[...], k1_ref[...], k2_ref[...]]
    vals = [v0_ref[...], v1_ref[...], v2_ref[...]]
    dk = [jnp.zeros((tok, HEAD_SIZE), jnp.float32) for _ in range(3)]
    dv = [jnp.zeros((tok, HEAD_SIZE), jnp.float32) for _ in range(3)]
    for j in range(share):
        qj = q_ref[:, j * HEAD_SIZE:(j + 1) * HEAD_SIZE]
        gj = g_ref[:, j * HEAD_SIZE:(j + 1) * HEAD_SIZE]
        scores = []
        for d in range(3):
            s = score_scale * lax.dot_general(qj, keys[d], NT, preferred_element_type=jnp.float32)
            scores.append(jnp.where(masks[d], s, -jnp.inf))
        m = jnp.max(scores[0], axis=1, keepdims=True)
        for d in range(1, 3):
            m = jnp.maximum(m, jnp.max(scores[d], axis=1, keepdims=True))
        weights = [jnp.exp(scores[d] - m) for d in range(3)]
        tot = jnp.zeros_like(m)
        for d in range(3):
            tot = tot + jnp.sum(weights[d], axis=1, keepdims=True)
        inv_tot = 1.0 / tot
        probs, dprobs = [], []
        delta = jnp.zeros_like(m)
        for d in range(3):
            p = weights[d] * inv_tot
            dp = lax.dot_general(gj, vals[d], NT, preferred_element_type=jnp.float32)
            delta = delta + jnp.sum(p * dp, axis=1, keepdims=True)
            probs.append(p)
            dprobs.append(dp)
        dq = jnp.zeros((tok, HEAD_SIZE), jnp.float32)
        for d in range(3):
            ds = (probs[d] * (dprobs[d] - delta)).astype(jnp.bfloat16)
            ph = probs[d].astype(jnp.bfloat16)
            dq = dq + jnp.dot(ds, keys[d], preferred_element_type=jnp.float32)
            dk[d] = dk[d] + lax.dot_general(ds, qj, TN, preferred_element_type=jnp.float32)
            dv[d] = dv[d] + lax.dot_general(ph, gj, TN, preferred_element_type=jnp.float32)
        dq_ref[:, j * HEAD_SIZE:(j + 1) * HEAD_SIZE] = score_scale * dq
    for d in range(3):
        dkv_refs[d][0] = score_scale * dk[d]
        dkv_refs[d][1] = dv[d]


def attend(rel, x_all, kv_blocks):
    tok = x_all.shape[0]
    kvcols = kv_blocks[0].shape[1] // 2
    groups = kvcols // HEAD_SIZE
    qblk = 2 * kvcols // groups
    col = lambda off: pl.BlockSpec((tok, HEAD_SIZE), lambda g: (0, off + g))
    qcol = lambda off: pl.BlockSpec((tok, qblk), lambda g: (0, off + g))
    kv_spec = pl.BlockSpec((2, tok, HEAD_SIZE), lambda g: (0, 0, g))
    return pl.pallas_call(
        attn_kernel,
        grid=(groups,),
        in_specs=[
            pl.BlockSpec((tok, 1), lambda g: (0, 0)),
            qcol(2 * kvcols // qblk),
            qcol(4 * kvcols // qblk),
            col(0),
            col(groups),
            col(0),
            col(groups),
            col(0),
            col(groups),
        ],
        out_specs=[pl.BlockSpec((tok, qblk), lambda g: (0, g)), kv_spec, kv_spec, kv_spec],
        out_shape=[
            jax.ShapeDtypeStruct((tok, 2 * kvcols), jnp.float32),
            jax.ShapeDtypeStruct((2, tok, kvcols), jnp.float32),
            jax.ShapeDtypeStruct((2, tok, kvcols), jnp.float32),
            jax.ShapeDtypeStruct((2, tok, kvcols), jnp.float32),
        ],
    )(rel, x_all, x_all, x_all, x_all, kv_blocks[0], kv_blocks[0], kv_blocks[1], kv_blocks[1])


def passed_along(block, axis, distance):
    devices = range(lax.axis_size(axis))
    route = [(i - distance, i) for i in devices if i - distance in devices]
    return lax.ppermute(block, axis, route)


def chunk_pass(x_in, rel, kv_cols, q_cols):
    tok_rows = rel.shape[0]
    x_all = lax.all_to_all(x_in, "head", split_axis=1, concat_axis=0, tiled=True)
    x_all = x_all.reshape(tok_rows, 2 * kv_cols + 2 * q_cols)
    kv_local = x_all[:, : 2 * kv_cols]
    if CHAIN:
        kv1 = passed_along(kv_local, "ctx", 1)
        kv2 = passed_along(kv1, "ctx", 1)
    else:
        kv2 = passed_along(kv_local, "ctx", 2)
        kv1 = passed_along(kv_local, "ctx", 1)
    dq, dkv0, dkv1, dkv2 = attend(rel, x_all, (kv1, kv2))
    if CHAIN:
        carried = passed_along(dkv2.astype(jnp.bfloat16), "ctx", -1)
        carried = passed_along((dkv1 + carried).astype(jnp.bfloat16), "ctx", -1)
        kv_total = dkv0 + carried
    else:
        kv_total = dkv0
        for distance, part in ((2, dkv2), (1, dkv1)):
            kv_total = kv_total + passed_along(part.astype(jnp.bfloat16), "ctx", -distance)
    out_loc = jnp.concatenate(
        [dq.astype(jnp.bfloat16), kv_total[0].astype(jnp.bfloat16), kv_total[1].astype(jnp.bfloat16)],
        axis=1,
    )[:, None]
    return lax.all_to_all(out_loc, "head", split_axis=0, concat_axis=1, tiled=True)


def local(queries, normed_key_state, value_state_rows, output_gradient, doc_start):
    heads_ax = lax.axis_size("head")
    rows_in = queries.shape[0]
    tok_rows = doc_start.shape[0]
    kv_cols = normed_key_state.shape[1] // (heads_ax * CHUNKS)
    q_cols = queries.shape[1] // (heads_ax * CHUNKS)
    shard_index = lax.axis_index("ctx")
    rel = (doc_start - shard_index * tok_rows).reshape(tok_rows, 1)
    parts = [
        normed_key_state.reshape(rows_in, heads_ax, CHUNKS, kv_cols),
        value_state_rows.reshape(rows_in, heads_ax, CHUNKS, kv_cols),
        queries.reshape(rows_in, heads_ax, CHUNKS, q_cols),
        output_gradient.reshape(rows_in, heads_ax, CHUNKS, q_cols),
    ]
    outs = []
    for chunk in range(CHUNKS):
        x_in = jnp.concatenate([p[:, :, chunk] for p in parts], axis=2)
        outs.append(chunk_pass(x_in, rel, kv_cols, q_cols))
    out = jnp.stack(outs, axis=2)
    grad_q = out[..., :q_cols].reshape(rows_in, heads_ax * CHUNKS * q_cols)
    grad_k = out[..., q_cols : q_cols + kv_cols].reshape(rows_in, heads_ax * CHUNKS * kv_cols)
    grad_v = out[..., q_cols + kv_cols :].reshape(rows_in, heads_ax * CHUNKS * kv_cols)
    return grad_q, grad_k, grad_v


def solution(mesh):
    placed = (
        P(("ctx", "head"), None),
        P(("ctx", "head"), None),
        P(("ctx", "head"), None),
        P(("ctx", "head"), None),
        P("ctx"),
    )
    return jax.shard_map(
        local,
        mesh=mesh,
        in_specs=placed,
        out_specs=(P(("ctx", "head"), None), P(("ctx", "head"), None), P(("ctx", "head"), None)),
        check_vma=False,
    )
```
